128 devices in a mesh: chain: 32 (over z, x, core), dp: 4 (over y).
Axes of the slice: x: 4, y: 4, z: 4, core: 2. Of those that a mesh axis runs over, the one named last changes fastest.
Arguments:
- hidden: bfloat16 [4, 4096, 4096], P('dp', 'chain'), may hold values from -6 to 6
- w_bc: bfloat16 [4096, 256], replicated, may hold values from -0.046875 to 0.046875
- xs: bfloat16 [4, 4096, 4096], P('dp', 'chain'), may hold values from -6 to 6
- dt_raw: float32 [4, 4096, 32], P('dp', 'chain'), may hold values from -4 to 4
- a_log: float32 [32], replicated, as said below
- d_out: bfloat16 [4, 4096, 4096], P('dp', 'chain'), may hold values from -6 to 6
Outputs:
- d_xs: bfloat16 [4, 4096, 4096], P('dp', 'chain')
- d_wbc: float32 [4096, 256], replicated
- d_alog: float32 [32], replicated
The draws below stay inside these ranges and needn't reach their ends.
Inputs may be any that keep to these rules, and one draw needn't show every extreme that they name: exp(a_log) lies between 0.3 / 4096 and 0.05.
All inputs are finite; a program needn't handle non-finite values.
Results may differ from the reference program's by a relative error of at most 0.0058.
Values sent between devices are 32-bit elements; how exact they have to be, the bound alone decides.
No kernel may reach another device: no remote copies, remote signals or barrier semaphores. Data moves between devices by JAX's collectives and lax.ppermute only.
A program may use at most 448 MiB of HBM per device.

```python
import jax
import jax.numpy as jnp
from jax import lax

D = 4096
HEADS = 32
HEAD_DIM = 128
STATE = 128
GROUP = 128
TOK_DEV = 128
STREAMS = 4
TOKENS = 4096
N_CHAIN = 32


def draw_a_log(key, part):
    first, second, third = jax.random.split(key, 3)
    total = TOKENS * 1.0
    lowest = jnp.log(0.3 / total)
    middle = jnp.log(2.8 / total)
    highest = jnp.log(0.05)
    share = 0.5
    slow = jax.random.uniform(first, (HEADS,)) < share
    slow_vals = lowest + (middle - lowest) * jax.random.uniform(second, (HEADS,))
    fast_vals = middle + (highest - middle) * jax.random.uniform(third, (HEADS,))
    return jnp.where(slow, slow_vals, fast_vals).astype(jnp.float32)


def levels(rng, shape, cuts, smallest, high):
    gain, own = 1.0, jax.random.fold_in(rng, 6)
    for dim, parts in cuts:
        heights = jnp.exp(jax.random.uniform(jax.random.fold_in(own, dim), (parts,), jnp.float32, smallest / len(cuts), high / len(cuts)))
        gain = gain * jnp.repeat(heights, shape[dim] // parts).reshape([-1 if axis == dim else 1 for axis in range(len(shape))])
    return gain


def gaussian(rng, dims, spread, bound, cuts=(), kind=jnp.bfloat16):
    loudness = levels(rng, dims, cuts, -0.22, 0.18) if cuts else 1.0
    result = jax.random.normal(rng, dims, jnp.float32) * spread * loudness
    return jnp.minimum(jnp.maximum(result, -bound), bound).astype(kind)


def setup_inputs(seed: int = 0) -> dict:
    seeds = jax.random.split(jax.random.key(seed), 7)
    hidden = gaussian(seeds[0], (STREAMS, TOKENS, D), 1.0, 6.0, ((0, 4), (1, 32)))
    w_bc = gaussian(seeds[1], (D, 2 * STATE), (4 * D) ** -0.5, 0.046875)
    xs = gaussian(seeds[2], (STREAMS, TOKENS, HEADS * HEAD_DIM), 1.0, 6.0, ((0, 4), (1, 32)))
    dt_raw = gaussian(seeds[3], (STREAMS, TOKENS, HEADS), 1.0, 4.0, ((0, 4), (1, 32)), jnp.float32)
    a_log = draw_a_log(jax.random.fold_in(seeds[6], 71), 0)
    d_out = gaussian(seeds[5], (STREAMS, TOKENS, HEADS * HEAD_DIM), 1.0, 6.0, ((0, 4), (1, 32)))
    return dict(hidden=hidden, w_bc=w_bc, xs=xs, dt_raw=dt_raw, a_log=a_log, d_out=d_out)


HIGH = lax.Precision.HIGHEST

def block_forward(bc, x, dt_raw, a_log, h_in):
    length = x.shape[0]
    heads = h_in.shape[0]
    width = h_in.shape[1]
    state = h_in.shape[2]
    blocks = length // GROUP
    step = jax.nn.softplus(dt_raw)
    logdec = -step * jnp.exp(a_log)[None, :]
    b_in = bc[:, :state].astype(jnp.float32).reshape(blocks, GROUP, state)
    c_out = bc[:, state:].astype(jnp.float32).reshape(blocks, GROUP, state)
    inputs = (x.astype(jnp.float32).reshape(length, heads, width) * step[:, :, None]).reshape(blocks, GROUP, heads, width)
    decays = jnp.transpose(logdec.reshape(blocks, GROUP, heads), (0, 2, 1))
    rows = jnp.arange(GROUP, dtype=jnp.int32)
    causal = rows[:, None] >= rows[None, :]
    cum = jnp.cumsum(decays, axis=2)
    diff = cum[:, :, :, None] - cum[:, :, None, :]
    weights = jnp.exp(jnp.where(causal[None, None, :, :], diff, -jnp.inf))
    scores = jnp.einsum('ktn,ksn->kts', c_out, b_in, precision=HIGH)
    mixing = weights * scores[:, None, :, :]
    y_intra = jnp.einsum('khts,kshp->kthp', mixing, inputs, precision=HIGH)
    ends = cum[:, :, -1]
    edge = jnp.concatenate([jnp.zeros((1, heads), jnp.float32), jnp.cumsum(ends, axis=0)], axis=0)
    tail = jnp.transpose(jnp.exp(ends[:, :, None] - cum), (0, 2, 1))
    fresh = jnp.einsum('kshp,ksn->khpn', inputs * tail[:, :, :, None], b_in, precision=HIGH)
    targets = jnp.arange(blocks + 1, dtype=jnp.int32)
    sources = jnp.arange(blocks, dtype=jnp.int32)
    before = sources[None, :] < targets[:, None]
    gap = edge[:, None, :] - edge[None, 1:, :]
    carry_weight = jnp.exp(jnp.where(before[:, :, None], gap, -jnp.inf))
    starts = jnp.einsum('kjh,jhpn->khpn', carry_weight, fresh, precision=HIGH) + jnp.exp(edge)[:, :, None, None] * h_in[None]
    y_inter = jnp.einsum('ktn,khpn->kthp', c_out, starts[:blocks], precision=HIGH) * jnp.exp(jnp.transpose(cum, (0, 2, 1)))[:, :, :, None]
    return ((y_intra + y_inter).reshape(length, heads * width), starts[blocks])

def reference(hidden, w_bc, xs, dt_raw, a_log, d_out):
    heads = a_log.shape[0]
    width = xs.shape[2] // heads
    state = w_bc.shape[1] // 2

    def one_stream(total, items):
        u, x, dtr, dy = items
        bc = jnp.dot(u, w_bc, preferred_element_type=jnp.float32).astype(jnp.bfloat16)

        def run(bc_all, x_all, alog):

            def block(h, pieces):
                bcb, xb, db = pieces
                y, h_next = block_forward(bcb, xb, db, alog, h)
                return (h_next, y)
            zero = jnp.zeros((heads, width, state), jnp.float32)
            _, ys = lax.scan(block, zero, (bc_all.reshape(N_CHAIN, TOK_DEV, 2 * state), x_all.reshape(N_CHAIN, TOK_DEV, heads * width), dtr.reshape(N_CHAIN, TOK_DEV, heads)))
            return ys.reshape(TOKENS, heads * width)
        _, pull = jax.vjp(run, bc, x, a_log)
        d_bc, d_x, d_al = pull(dy.astype(jnp.float32))
        d_w = lax.dot_general(u, d_bc, (((0,), (0,)), ((), ())), preferred_element_type=jnp.float32)
        return ((total[0] + d_w, total[1] + d_al), d_x)
    init = (jnp.zeros((w_bc.shape[0], 2 * state), jnp.float32), jnp.zeros((heads,), jnp.float32))
    sums, d_xs = lax.scan(one_stream, init, (hidden, xs, dt_raw, d_out))
    return (d_xs, sums[0], sums[1])
```

```python
import jax
import jax.numpy as jnp
from jax import lax
from jax.sharding import PartitionSpec as P

GROUP = 128


HIGH = lax.Precision.HIGHEST


def exchange(log_total, own_state, back_term):
    count, mine = (lax.axis_size("chain"), lax.axis_index("chain"))
    heads, width, state = own_state.shape
    per = heads // count
    both = jnp.stack([own_state, back_term], axis=1)
    parts = lax.all_to_all(both, "chain", 0, 0, tiled=True).reshape(count, per, 2, width * state)
    logs = lax.all_gather(log_total, "chain")
    mine_logs = lax.dynamic_slice_in_dim(logs, mine * per, per, axis=1)
    edge = jnp.cumsum(mine_logs, axis=0) - mine_logs
    after = edge + mine_logs
    pos = jnp.arange(count, dtype=jnp.int32)
    earlier = pos[None, :] < pos[:, None]
    fwd_w = jnp.exp(jnp.where(earlier[:, :, None], edge[:, None, :] - after[None, :, :], -jnp.inf))
    bwd_w = jnp.exp(jnp.where(earlier.T[:, :, None], edge[None, :, :] - after[:, None, :], -jnp.inf))
    inc = jnp.einsum("djh,jhx->dhx", fwd_w, parts[:, :, 0], precision=HIGH)
    out = jnp.einsum("djh,jhx->dhx", bwd_w, parts[:, :, 1], precision=HIGH)
    res = jnp.stack([inc, out], axis=2).reshape(count * per, 2, width, state)
    back = lax.all_to_all(res, "chain", 0, 0, tiled=True)
    return back[:, 0], back[:, 1]


def block_forward(bc, x, dt_raw, a_log, h_in):
    length = x.shape[0]
    heads = h_in.shape[0]
    width = h_in.shape[1]
    state = h_in.shape[2]
    blocks = length // GROUP
    step = jax.nn.softplus(dt_raw)
    logdec = -step * jnp.exp(a_log)[None, :]
    b_in = bc[:, :state].astype(jnp.float32).reshape(blocks, GROUP, state)
    c_out = bc[:, state:].astype(jnp.float32).reshape(blocks, GROUP, state)
    inputs = (x.astype(jnp.float32).reshape(length, heads, width) * step[:, :, None]).reshape(
        blocks, GROUP, heads, width
    )
    decays = jnp.transpose(logdec.reshape(blocks, GROUP, heads), (0, 2, 1))
    rows = jnp.arange(GROUP, dtype=jnp.int32)
    causal = rows[:, None] >= rows[None, :]
    cum = jnp.cumsum(decays, axis=2)
    diff = cum[:, :, :, None] - cum[:, :, None, :]
    weights = jnp.exp(jnp.where(causal[None, None, :, :], diff, -jnp.inf))
    scores = jnp.einsum("ktn,ksn->kts", c_out, b_in, precision=HIGH)
    mixing = weights * scores[:, None, :, :]
    y_intra = jnp.einsum("khts,kshp->kthp", mixing, inputs, precision=HIGH)
    ends = cum[:, :, -1]
    edge = jnp.concatenate([jnp.zeros((1, heads), jnp.float32), jnp.cumsum(ends, axis=0)], axis=0)
    tail = jnp.transpose(jnp.exp(ends[:, :, None] - cum), (0, 2, 1))
    fresh = jnp.einsum("kshp,ksn->khpn", inputs * tail[:, :, :, None], b_in, precision=HIGH)
    targets = jnp.arange(blocks + 1, dtype=jnp.int32)
    sources = jnp.arange(blocks, dtype=jnp.int32)
    before = sources[None, :] < targets[:, None]
    gap = edge[:, None, :] - edge[None, 1:, :]
    carry_weight = jnp.exp(jnp.where(before[:, :, None], gap, -jnp.inf))
    starts = (
        jnp.einsum("kjh,jhpn->khpn", carry_weight, fresh, precision=HIGH)
        + jnp.exp(edge)[:, :, None, None] * h_in[None]
    )
    y_inter = (
        jnp.einsum("ktn,khpn->kthp", c_out, starts[:blocks], precision=HIGH)
        * jnp.exp(jnp.transpose(cum, (0, 2, 1)))[:, :, :, None]
    )
    return ((y_intra + y_inter).reshape(length, heads * width), starts[blocks])


def per_device(hidden, w_bc, xs, dt_raw, a_log, d_out):
    tokens_here = hidden[0]
    channels = xs[0]
    step_raw = dt_raw[0]
    upstream = d_out[0].astype(jnp.float32)
    heads = a_log.shape[0]
    width = channels.shape[1] // heads
    state = w_bc.shape[1] // 2
    length = channels.shape[0]
    bc = jnp.dot(tokens_here, w_bc, preferred_element_type=jnp.float32).astype(jnp.bfloat16)
    step_sizes = jax.nn.softplus(step_raw)
    log_decay = -step_sizes * jnp.exp(a_log)[None, :]
    running = jnp.cumsum(log_decay, axis=0)
    b_rows = bc[:, :state].astype(jnp.float32)
    c_rows = bc[:, state:].astype(jnp.float32)
    tail_weight = jnp.exp(running[-1:, :] - running) * step_sizes
    weighted = channels.astype(jnp.float32).reshape(length, heads, width) * tail_weight[:, :, None]
    own_state = jnp.einsum("thp,tn->hpn", weighted, b_rows, precision=HIGH)
    scaled_grad = upstream.reshape(length, heads, width) * jnp.exp(running)[:, :, None]
    back_term = jnp.einsum("thp,tn->hpn", scaled_grad, c_rows, precision=HIGH)
    incoming, outgoing_grad = exchange(running[-1], own_state, back_term)

    def whole_block(bc_in, x_in, alog_in):
        return block_forward(bc_in, x_in, step_raw, alog_in, incoming)

    _, pull_all = jax.vjp(whole_block, bc, channels, a_log)
    d_bc, d_x, d_rate = pull_all((upstream, outgoing_grad))
    d_weight = lax.dot_general(
        tokens_here, d_bc, (((0,), (0,)), ((), ())), preferred_element_type=jnp.float32
    )
    d_wbc, d_alog = lax.psum((d_weight, d_rate), ("chain", "dp"))
    return (d_x[None], d_wbc, d_alog)


def solution(mesh):
    return jax.shard_map(
        per_device,
        mesh=mesh,
        in_specs=(
            P("dp", "chain", None),
            P(),
            P("dp", "chain", None),
            P("dp", "chain", None),
            P(),
            P("dp", "chain", None),
        ),
        out_specs=(P("dp", "chain", None), P(), P()),
        check_vma=False,
    )
```

```python
import jax
import jax.numpy as jnp
from jax import lax
from jax.sharding import PartitionSpec as P

GROUP = 128


HIGH = lax.Precision.HIGHEST


def exchange(log_total, own_state, back_term):
    count, mine = (lax.axis_size("chain"), lax.axis_index("chain"))
    heads, width, state = own_state.shape
    per = heads // count
    size = width * state
    both = jnp.concatenate(
        [
            own_state.reshape(heads, size),
            back_term.reshape(heads, size),
            jnp.broadcast_to(log_total[:, None], (heads, 128)),
        ],
        axis=1,
    )
    sent = lax.all_to_all(both, "chain", 0, 0, tiled=True).reshape(count, per, 2 * size + 128)
    parts = sent[:, :, : 2 * size].reshape(count, per, 2, size)
    mine_logs = sent[:, :, 2 * size]
    edge = jnp.cumsum(mine_logs, axis=0) - mine_logs
    after = edge + mine_logs
    pos = jnp.arange(count, dtype=jnp.int32)
    earlier = pos[None, :] < pos[:, None]
    fwd_w = jnp.exp(jnp.where(earlier[:, :, None], edge[:, None, :] - after[None, :, :], -jnp.inf))
    bwd_w = jnp.exp(jnp.where(earlier.T[:, :, None], edge[None, :, :] - after[:, None, :], -jnp.inf))
    inc = jnp.einsum("djh,jhx->dhx", fwd_w, parts[:, :, 0], precision=HIGH)
    out = jnp.einsum("djh,jhx->dhx", bwd_w, parts[:, :, 1], precision=HIGH)
    res = jnp.stack([inc, out], axis=2).reshape(count * per, 2, width, state)
    back = lax.all_to_all(res, "chain", 0, 0, tiled=True)
    return back[:, 0], back[:, 1]


def block_forward(bc, x, dt_raw, a_log, h_in):
    length = x.shape[0]
    heads = h_in.shape[0]
    width = h_in.shape[1]
    state = h_in.shape[2]
    blocks = length // GROUP
    step = jax.nn.softplus(dt_raw)
    logdec = -step * jnp.exp(a_log)[None, :]
    b_in = bc[:, :state].astype(jnp.float32).reshape(blocks, GROUP, state)
    c_out = bc[:, state:].astype(jnp.float32).reshape(blocks, GROUP, state)
    inputs = (x.astype(jnp.float32).reshape(length, heads, width) * step[:, :, None]).reshape(
        blocks, GROUP, heads, width
    )
    decays = jnp.transpose(logdec.reshape(blocks, GROUP, heads), (0, 2, 1))
    rows = jnp.arange(GROUP, dtype=jnp.int32)
    causal = rows[:, None] >= rows[None, :]
    cum = jnp.cumsum(decays, axis=2)
    diff = cum[:, :, :, None] - cum[:, :, None, :]
    weights = jnp.exp(jnp.where(causal[None, None, :, :], diff, -jnp.inf))
    scores = jnp.einsum("ktn,ksn->kts", c_out, b_in, precision=HIGH)
    mixing = weights * scores[:, None, :, :]
    y_intra = jnp.einsum("khts,kshp->kthp", mixing, inputs, precision=HIGH)
    ends = cum[:, :, -1]
    edge = jnp.concatenate([jnp.zeros((1, heads), jnp.float32), jnp.cumsum(ends, axis=0)], axis=0)
    tail = jnp.transpose(jnp.exp(ends[:, :, None] - cum), (0, 2, 1))
    fresh = jnp.einsum("kshp,ksn->khpn", inputs * tail[:, :, :, None], b_in, precision=HIGH)
    targets = jnp.arange(blocks + 1, dtype=jnp.int32)
    sources = jnp.arange(blocks, dtype=jnp.int32)
    before = sources[None, :] < targets[:, None]
    gap = edge[:, None, :] - edge[None, 1:, :]
    carry_weight = jnp.exp(jnp.where(before[:, :, None], gap, -jnp.inf))
    starts = (
        jnp.einsum("kjh,jhpn->khpn", carry_weight, fresh, precision=HIGH)
        + jnp.exp(edge)[:, :, None, None] * h_in[None]
    )
    y_inter = (
        jnp.einsum("ktn,khpn->kthp", c_out, starts[:blocks], precision=HIGH)
        * jnp.exp(jnp.transpose(cum, (0, 2, 1)))[:, :, :, None]
    )
    return ((y_intra + y_inter).reshape(length, heads * width), starts[blocks])


def per_device(hidden, w_bc, xs, dt_raw, a_log, d_out):
    tokens_here = hidden[0]
    channels = xs[0]
    step_raw = dt_raw[0]
    upstream = d_out[0].astype(jnp.float32)
    heads = a_log.shape[0]
    width = channels.shape[1] // heads
    state = w_bc.shape[1] // 2
    length = channels.shape[0]
    bc = jnp.dot(tokens_here, w_bc, preferred_element_type=jnp.float32).astype(jnp.bfloat16)
    step_sizes = jax.nn.softplus(step_raw)
    log_decay = -step_sizes * jnp.exp(a_log)[None, :]
    running = jnp.cumsum(log_decay, axis=0)
    b_rows = bc[:, :state].astype(jnp.float32)
    c_rows = bc[:, state:].astype(jnp.float32)
    tail_weight = jnp.exp(running[-1:, :] - running) * step_sizes
    weighted = channels.astype(jnp.float32).reshape(length, heads, width) * tail_weight[:, :, None]
    own_state = jnp.einsum("thp,tn->hpn", weighted, b_rows, precision=HIGH)
    scaled_grad = upstream.reshape(length, heads, width) * jnp.exp(running)[:, :, None]
    back_term = jnp.einsum("thp,tn->hpn", scaled_grad, c_rows, precision=HIGH)
    incoming, outgoing_grad = exchange(running[-1], own_state, back_term)

    def whole_block(bc_in, x_in, alog_in):
        return block_forward(bc_in, x_in, step_raw, alog_in, incoming)

    _, pull_all = jax.vjp(whole_block, bc, channels, a_log)
    d_bc, d_x, d_rate = pull_all((upstream, outgoing_grad))
    d_weight = lax.dot_general(
        tokens_here, d_bc, (((0,), (0,)), ((), ())), preferred_element_type=jnp.float32
    )
    rows = d_weight.shape[0]
    rate_rows = jnp.zeros((8, d_weight.shape[1]), jnp.float32).at[0, : heads].set(d_rate)
    summed = lax.psum(jnp.concatenate([d_weight, rate_rows], axis=0), ("chain", "dp"))
    return (d_x[None], summed[:rows], summed[rows, :heads])


def solution(mesh):
    return jax.shard_map(
        per_device,
        mesh=mesh,
        in_specs=(
            P("dp", "chain", None),
            P(),
            P("dp", "chain", None),
            P("dp", "chain", None),
            P(),
            P("dp", "chain", None),
        ),
        out_specs=(P("dp", "chain", None), P(), P()),
        check_vma=False,
    )
```

```python
import jax
import jax.numpy as jnp
from jax import lax
from jax.sharding import PartitionSpec as P

GROUP = 128


HIGH = lax.Precision.HIGHEST


def exchange(log_total, own_state, back_term):
    count, mine = (lax.axis_size("chain"), lax.axis_index("chain"))
    heads, width, state = own_state.shape
    per = heads // count
    both = jnp.stack([own_state, back_term], axis=1)
    parts = lax.all_to_all(both, "chain", 0, 0, tiled=True).reshape(count, per, 2, width * state)
    logs = lax.all_gather(log_total, "chain")
    mine_logs = lax.dynamic_slice_in_dim(logs, mine * per, per, axis=1)
    edge = jnp.cumsum(mine_logs, axis=0) - mine_logs
    after = edge + mine_logs
    pos = jnp.arange(count, dtype=jnp.int32)
    earlier = pos[None, :] < pos[:, None]
    fwd_w = jnp.exp(jnp.where(earlier[:, :, None], edge[:, None, :] - after[None, :, :], -jnp.inf))
    bwd_w = jnp.exp(jnp.where(earlier.T[:, :, None], edge[None, :, :] - after[:, None, :], -jnp.inf))
    inc = jnp.einsum("djh,jhx->dhx", fwd_w, parts[:, :, 0], precision=HIGH)
    out = jnp.einsum("djh,jhx->dhx", bwd_w, parts[:, :, 1], precision=HIGH)
    res = jnp.stack([inc, out], axis=2).reshape(count * per, 2, width, state)
    back = lax.all_to_all(res, "chain", 0, 0, tiled=True)
    return back[:, 0], back[:, 1]


def block_forward(bc, x, dt_raw, a_log, h_in):
    length = x.shape[0]
    heads = h_in.shape[0]
    width = h_in.shape[1]
    state = h_in.shape[2]
    step = jax.nn.softplus(dt_raw)
    logdec = -step * jnp.exp(a_log)[None, :]
    b_in = bc[:, :state].astype(jnp.float32)
    c_out = bc[:, state:].astype(jnp.float32)
    inputs = x.astype(jnp.float32).reshape(length, heads, width) * step[:, :, None]
    decays = jnp.transpose(logdec, (1, 0))
    rows = jnp.arange(length, dtype=jnp.int32)
    causal = rows[:, None] >= rows[None, :]
    cum = jnp.cumsum(decays, axis=1)
    diff = cum[:, :, None] - cum[:, None, :]
    weights = jnp.exp(jnp.where(causal[None, :, :], diff, -jnp.inf))
    scores = jnp.einsum("tn,sn->ts", c_out, b_in, precision=HIGH)
    mixing = weights * scores[None, :, :]
    y_intra = jnp.einsum("hts,shp->thp", mixing, inputs, precision=HIGH)
    ends = cum[:, -1]
    tail = jnp.transpose(jnp.exp(ends[:, None] - cum), (1, 0))
    fresh = jnp.einsum("shp,sn->hpn", inputs * tail[:, :, None], b_in, precision=HIGH)
    h_end = fresh + jnp.exp(ends)[:, None, None] * h_in
    y_inter = (
        jnp.einsum("tn,hpn->thp", c_out, h_in, precision=HIGH)
        * jnp.exp(jnp.transpose(cum, (1, 0)))[:, :, None]
    )
    return ((y_intra + y_inter).reshape(length, heads * width), h_end)


def per_device(hidden, w_bc, xs, dt_raw, a_log, d_out):
    tokens_here = hidden[0]
    channels = xs[0]
    step_raw = dt_raw[0]
    upstream = d_out[0].astype(jnp.float32)
    heads = a_log.shape[0]
    width = channels.shape[1] // heads
    state = w_bc.shape[1] // 2
    length = channels.shape[0]
    bc = jnp.dot(tokens_here, w_bc, preferred_element_type=jnp.float32).astype(jnp.bfloat16)
    step_sizes = jax.nn.softplus(step_raw)
    log_decay = -step_sizes * jnp.exp(a_log)[None, :]
    running = jnp.cumsum(log_decay, axis=0)
    b_rows = bc[:, :state].astype(jnp.float32)
    c_rows = bc[:, state:].astype(jnp.float32)
    tail_weight = jnp.exp(running[-1:, :] - running) * step_sizes
    weighted = channels.astype(jnp.float32).reshape(length, heads, width) * tail_weight[:, :, None]
    own_state = jnp.einsum("thp,tn->hpn", weighted, b_rows, precision=HIGH)
    scaled_grad = upstream.reshape(length, heads, width) * jnp.exp(running)[:, :, None]
    back_term = jnp.einsum("thp,tn->hpn", scaled_grad, c_rows, precision=HIGH)
    incoming, outgoing_grad = exchange(running[-1], own_state, back_term)

    def whole_block(bc_in, x_in, alog_in):
        return block_forward(bc_in, x_in, step_raw, alog_in, incoming)

    _, pull_all = jax.vjp(whole_block, bc, channels, a_log)
    d_bc, d_x, d_rate = pull_all((upstream, outgoing_grad))
    d_weight = lax.dot_general(
        tokens_here, d_bc, (((0,), (0,)), ((), ())), preferred_element_type=jnp.float32
    )
    d_wbc, d_alog = lax.psum((d_weight, d_rate), ("chain", "dp"))
    return (d_x[None], d_wbc, d_alog)


def solution(mesh):
    return jax.shard_map(
        per_device,
        mesh=mesh,
        in_specs=(
            P("dp", "chain", None),
            P(),
            P("dp", "chain", None),
            P("dp", "chain", None),
            P(),
            P("dp", "chain", None),
        ),
        out_specs=(P("dp", "chain", None), P(), P()),
        check_vma=False,
    )
```

```python
import jax
import jax.numpy as jnp
from jax import lax
from jax.sharding import PartitionSpec as P

GROUP = 128


HIGH = lax.Precision.HIGHEST


def exchange(log_total, own_state, back_term):
    count, mine = (lax.axis_size("chain"), lax.axis_index("chain"))
    heads, width, state = own_state.shape
    per = heads // count
    marks = jnp.broadcast_to(log_total[:, None, None], (heads, 8, state))
    both = jnp.stack(
        [jnp.concatenate([own_state, marks], axis=1), jnp.concatenate([back_term, marks], axis=1)], axis=1
    )
    sent = lax.all_to_all(both, "chain", 0, 0, tiled=True).reshape(count, per, 2, width + 8, state)
    parts = sent[:, :, :, :width].reshape(count, per, 2, width * state)
    mine_logs = sent[:, :, 0, width, 0]
    edge = jnp.cumsum(mine_logs, axis=0) - mine_logs
    after = edge + mine_logs
    pos = jnp.arange(count, dtype=jnp.int32)
    earlier = pos[None, :] < pos[:, None]
    fwd_w = jnp.exp(jnp.where(earlier[:, :, None], edge[:, None, :] - after[None, :, :], -jnp.inf))
    bwd_w = jnp.exp(jnp.where(earlier.T[:, :, None], edge[None, :, :] - after[:, None, :], -jnp.inf))
    inc = jnp.einsum("djh,jhx->dhx", fwd_w, parts[:, :, 0], precision=HIGH)
    out = jnp.einsum("djh,jhx->dhx", bwd_w, parts[:, :, 1], precision=HIGH)
    res = jnp.stack([inc, out], axis=2).reshape(count * per, 2, width, state)
    back = lax.all_to_all(res, "chain", 0, 0, tiled=True)
    return back[:, 0], back[:, 1]


def block_forward(bc, x, dt_raw, a_log, h_in):
    length = x.shape[0]
    heads = h_in.shape[0]
    width = h_in.shape[1]
    state = h_in.shape[2]
    step = jax.nn.softplus(dt_raw)
    logdec = -step * jnp.exp(a_log)[None, :]
    b_in = bc[:, :state].astype(jnp.float32)
    c_out = bc[:, state:].astype(jnp.float32)
    inputs = x.astype(jnp.float32).reshape(length, heads, width) * step[:, :, None]
    decays = jnp.transpose(logdec, (1, 0))
    rows = jnp.arange(length, dtype=jnp.int32)
    causal = rows[:, None] >= rows[None, :]
    cum = jnp.cumsum(decays, axis=1)
    diff = cum[:, :, None] - cum[:, None, :]
    weights = jnp.exp(jnp.where(causal[None, :, :], diff, -jnp.inf))
    scores = jnp.einsum("tn,sn->ts", c_out, b_in, precision=HIGH)
    mixing = weights * scores[None, :, :]
    y_intra = jnp.einsum("hts,shp->thp", mixing, inputs, precision=HIGH)
    ends = cum[:, -1]
    tail = jnp.transpose(jnp.exp(ends[:, None] - cum), (1, 0))
    fresh = jnp.einsum("shp,sn->hpn", inputs * tail[:, :, None], b_in, precision=HIGH)
    h_end = fresh + jnp.exp(ends)[:, None, None] * h_in
    y_inter = (
        jnp.einsum("tn,hpn->thp", c_out, h_in, precision=HIGH)
        * jnp.exp(jnp.transpose(cum, (1, 0)))[:, :, None]
    )
    return ((y_intra + y_inter).reshape(length, heads * width), h_end)


def per_device(hidden, w_bc, xs, dt_raw, a_log, d_out):
    tokens_here = hidden[0]
    channels = xs[0]
    step_raw = dt_raw[0]
    upstream = d_out[0].astype(jnp.float32)
    heads = a_log.shape[0]
    width = channels.shape[1] // heads
    state = w_bc.shape[1] // 2
    length = channels.shape[0]
    bc = jnp.dot(tokens_here, w_bc, preferred_element_type=jnp.float32).astype(jnp.bfloat16)
    step_sizes = jax.nn.softplus(step_raw)
    log_decay = -step_sizes * jnp.exp(a_log)[None, :]
    running = jnp.cumsum(log_decay, axis=0)
    b_rows = bc[:, :state].astype(jnp.float32)
    c_rows = bc[:, state:].astype(jnp.float32)
    tail_weight = jnp.exp(running[-1:, :] - running) * step_sizes
    weighted = channels.astype(jnp.float32).reshape(length, heads, width) * tail_weight[:, :, None]
    own_state = jnp.einsum("thp,tn->hpn", weighted, b_rows, precision=HIGH)
    scaled_grad = upstream.reshape(length, heads, width) * jnp.exp(running)[:, :, None]
    back_term = jnp.einsum("thp,tn->hpn", scaled_grad, c_rows, precision=HIGH)
    incoming, outgoing_grad = exchange(running[-1], own_state, back_term)

    def whole_block(bc_in, x_in, alog_in):
        return block_forward(bc_in, x_in, step_raw, alog_in, incoming)

    _, pull_all = jax.vjp(whole_block, bc, channels, a_log)
    d_bc, d_x, d_rate = pull_all((upstream, outgoing_grad))
    d_weight = lax.dot_general(
        tokens_here, d_bc, (((0,), (0,)), ((), ())), preferred_element_type=jnp.float32
    )
    d_wbc, d_alog = lax.psum((d_weight, d_rate), ("chain", "dp"))
    return (d_x[None], d_wbc, d_alog)


def solution(mesh):
    return jax.shard_map(
        per_device,
        mesh=mesh,
        in_specs=(
            P("dp", "chain", None),
            P(),
            P("dp", "chain", None),
            P("dp", "chain", None),
            P(),
            P("dp", "chain", None),
        ),
        out_specs=(P("dp", "chain", None), P(), P()),
        check_vma=False,
    )
```

```python
import jax
import jax.numpy as jnp
from jax import lax
from jax.sharding import PartitionSpec as P

GROUP = 128


HIGH = lax.Precision.HIGHEST


def exchange(log_total, own_state, back_term):
    count, mine = (lax.axis_size("chain"), lax.axis_index("chain"))
    heads, width, state = own_state.shape
    per = heads // count
    marks = jnp.broadcast_to(log_total[:, None, None], (heads, 8, state))
    both = jnp.stack(
        [jnp.concatenate([own_state, marks], axis=1), jnp.concatenate([back_term, marks], axis=1)], axis=1
    )
    sent = lax.all_to_all(both, "chain", 0, 0, tiled=True).reshape(count, per, 2, width + 8, state)
    parts = sent[:, :, :, :width].reshape(count, per, 2, width * state)
    mine_logs = sent[:, :, 0, width, 0]
    edge = jnp.cumsum(mine_logs, axis=0) - mine_logs
    after = edge + mine_logs
    pos = jnp.arange(count, dtype=jnp.int32)
    earlier = pos[None, :] < pos[:, None]
    fwd_w = jnp.exp(jnp.where(earlier[:, :, None], edge[:, None, :] - after[None, :, :], -jnp.inf))
    bwd_w = jnp.exp(jnp.where(earlier.T[:, :, None], edge[None, :, :] - after[:, None, :], -jnp.inf))
    inc = jnp.einsum("djh,jhx->dhx", fwd_w, parts[:, :, 0], precision=HIGH)
    out = jnp.einsum("djh,jhx->dhx", bwd_w, parts[:, :, 1], precision=HIGH)
    res = jnp.stack([inc, out], axis=2).reshape(count * per, 2, width, state)
    back = lax.all_to_all(res, "chain", 0, 0, tiled=True)
    return back[:, 0], back[:, 1]


def block_forward(bc, x, dt_raw, a_log, h_in):
    length = x.shape[0]
    heads = h_in.shape[0]
    width = h_in.shape[1]
    state = h_in.shape[2]
    step = jax.nn.softplus(dt_raw)
    logdec = -step * jnp.exp(a_log)[None, :]
    b_in = bc[:, :state].astype(jnp.float32)
    c_out = bc[:, state:].astype(jnp.float32)
    inputs = x.astype(jnp.float32).reshape(length, heads, width) * step[:, :, None]
    decays = jnp.transpose(logdec, (1, 0))
    rows = jnp.arange(length, dtype=jnp.int32)
    causal = rows[:, None] >= rows[None, :]
    cum = jnp.cumsum(decays, axis=1)
    diff = cum[:, :, None] - cum[:, None, :]
    weights = jnp.exp(jnp.where(causal[None, :, :], diff, -jnp.inf))
    scores = jnp.einsum("tn,sn->ts", c_out, b_in, precision=HIGH)
    mixing = weights * scores[None, :, :]
    y_intra = jnp.einsum("hts,shp->thp", mixing, inputs, precision=HIGH)
    ends = cum[:, -1]
    tail = jnp.transpose(jnp.exp(ends[:, None] - cum), (1, 0))
    fresh = jnp.einsum("shp,sn->hpn", inputs * tail[:, :, None], b_in, precision=HIGH)
    h_end = fresh + jnp.exp(ends)[:, None, None] * h_in
    y_inter = (
        jnp.einsum("tn,hpn->thp", c_out, h_in, precision=HIGH)
        * jnp.exp(jnp.transpose(cum, (1, 0)))[:, :, None]
    )
    return ((y_intra + y_inter).reshape(length, heads * width), h_end)


def per_device(hidden, w_bc, xs, dt_raw, a_log, d_out):
    tokens_here = hidden[0]
    channels = xs[0]
    step_raw = dt_raw[0]
    upstream = d_out[0].astype(jnp.float32)
    heads = a_log.shape[0]
    width = channels.shape[1] // heads
    state = w_bc.shape[1] // 2
    length = channels.shape[0]
    bc = jnp.dot(tokens_here, w_bc, preferred_element_type=jnp.float32).astype(jnp.bfloat16)
    step_sizes = jax.nn.softplus(step_raw)
    log_decay = -step_sizes * jnp.exp(a_log)[None, :]
    running = jnp.cumsum(log_decay, axis=0)
    b_rows = bc[:, :state].astype(jnp.float32)
    c_rows = bc[:, state:].astype(jnp.float32)
    tail_weight = jnp.exp(running[-1:, :] - running) * step_sizes
    weighted = channels.astype(jnp.float32).reshape(length, heads, width) * tail_weight[:, :, None]
    own_state = jnp.einsum("thp,tn->hpn", weighted, b_rows, precision=HIGH)
    scaled_grad = upstream.reshape(length, heads, width) * jnp.exp(running)[:, :, None]
    back_term = jnp.einsum("thp,tn->hpn", scaled_grad, c_rows, precision=HIGH)
    incoming, outgoing_grad = exchange(running[-1], own_state, back_term)

    def whole_block(bc_in, x_in, alog_in):
        return block_forward(bc_in, x_in, step_raw, alog_in, incoming)

    _, pull_all = jax.vjp(whole_block, bc, channels, a_log)
    d_bc, d_x, d_rate = pull_all((upstream, outgoing_grad))
    d_weight = lax.dot_general(
        tokens_here, d_bc, (((0,), (0,)), ((), ())), preferred_element_type=jnp.float32
    )
    axes = ("chain", "dp")
    total = lax.axis_size(axes)
    rows, cols = d_weight.shape
    chunk = rows // total
    rate_rows = jnp.zeros((8, cols), jnp.float32).at[0, :heads].set(d_rate)
    parcel = jnp.concatenate(
        [d_weight.reshape(total, chunk, cols), jnp.broadcast_to(rate_rows[None], (total, 8, cols))], axis=1
    )
    pieces = lax.all_to_all(parcel, axes, 0, 0, tiled=True)
    mine_sum = jnp.sum(pieces, axis=0)
    spread = jnp.broadcast_to(mine_sum[None], (total, chunk + 8, cols))
    gathered = lax.all_to_all(spread, axes, 0, 0, tiled=True)
    d_wbc = gathered[:, :chunk].reshape(rows, cols)
    d_alog = gathered[0, chunk, :heads]
    return (d_x[None], d_wbc, d_alog)


def solution(mesh):
    return jax.shard_map(
        per_device,
        mesh=mesh,
        in_specs=(
            P("dp", "chain", None),
            P(),
            P("dp", "chain", None),
            P("dp", "chain", None),
            P(),
            P("dp", "chain", None),
        ),
        out_specs=(P("dp", "chain", None), P(), P()),
        check_vma=False,
    )
```

```python
import jax
import jax.numpy as jnp
from jax import lax
from jax.sharding import PartitionSpec as P

GROUP = 128


HIGH = lax.Precision.HIGHEST


def exchange(log_total, own_state, back_term):
    count, mine = (lax.axis_size("chain"), lax.axis_index("chain"))
    heads, width, state = own_state.shape
    per = heads // count
    marks = jnp.broadcast_to(log_total[:, None, None], (heads, 8, state))
    both = jnp.stack(
        [jnp.concatenate([own_state, marks], axis=1), jnp.concatenate([back_term, marks], axis=1)], axis=1
    )
    sent = lax.all_to_all(both, "chain", 0, 0, tiled=True).reshape(count, per, 2, width + 8, state)
    parts = sent[:, :, :, :width]
    mine_logs = sent[:, :, 0, width, 0]
    edge = jnp.cumsum(mine_logs, axis=0) - mine_logs
    after = edge + mine_logs
    pos = jnp.arange(count, dtype=jnp.int32)
    earlier = pos[None, :] < pos[:, None]
    fwd_w = jnp.exp(jnp.where(earlier[:, :, None], edge[:, None, :] - after[None, :, :], -jnp.inf))
    bwd_w = jnp.exp(jnp.where(earlier.T[:, :, None], edge[None, :, :] - after[:, None, :], -jnp.inf))
    inc = jnp.einsum("djh,jhpn->dhpn", fwd_w, parts[:, :, 0], precision=HIGH)
    out = jnp.einsum("djh,jhpn->dhpn", bwd_w, parts[:, :, 1], precision=HIGH)
    res = jnp.stack([inc, out], axis=2).reshape(count * per, 2, width, state)
    back = lax.all_to_all(res, "chain", 0, 0, tiled=True)
    return back[:, 0], back[:, 1]


def block_forward(bc, x, dt_raw, a_log, h_in):
    length = x.shape[0]
    heads = h_in.shape[0]
    width = h_in.shape[1]
    state = h_in.shape[2]
    step = jax.nn.softplus(dt_raw)
    logdec = -step * jnp.exp(a_log)[None, :]
    b_in = bc[:, :state].astype(jnp.float32)
    c_out = bc[:, state:].astype(jnp.float32)
    inputs = x.astype(jnp.float32).reshape(length, heads, width) * step[:, :, None]
    decays = jnp.transpose(logdec, (1, 0))
    rows = jnp.arange(length, dtype=jnp.int32)
    causal = rows[:, None] >= rows[None, :]
    cum = jnp.cumsum(decays, axis=1)
    diff = cum[:, :, None] - cum[:, None, :]
    weights = jnp.exp(jnp.where(causal[None, :, :], diff, -jnp.inf))
    scores = jnp.einsum("tn,sn->ts", c_out, b_in, precision=HIGH)
    mixing = weights * scores[None, :, :]
    y_intra = jnp.einsum("hts,shp->thp", mixing, inputs, precision=HIGH)
    ends = cum[:, -1]
    tail = jnp.transpose(jnp.exp(ends[:, None] - cum), (1, 0))
    fresh = jnp.einsum("shp,sn->hpn", inputs * tail[:, :, None], b_in, precision=HIGH)
    h_end = fresh + jnp.exp(ends)[:, None, None] * h_in
    y_inter = (
        jnp.einsum("tn,hpn->thp", c_out, h_in, precision=HIGH)
        * jnp.exp(jnp.transpose(cum, (1, 0)))[:, :, None]
    )
    return ((y_intra + y_inter).reshape(length, heads * width), h_end)


def per_device(hidden, w_bc, xs, dt_raw, a_log, d_out):
    tokens_here = hidden[0]
    channels = xs[0]
    step_raw = dt_raw[0]
    upstream = d_out[0].astype(jnp.float32)
    heads = a_log.shape[0]
    width = channels.shape[1] // heads
    state = w_bc.shape[1] // 2
    length = channels.shape[0]
    bc = jnp.dot(tokens_here, w_bc, preferred_element_type=jnp.float32).astype(jnp.bfloat16)
    step_sizes = jax.nn.softplus(step_raw)
    log_decay = -step_sizes * jnp.exp(a_log)[None, :]
    running = jnp.cumsum(log_decay, axis=0)
    b_rows = bc[:, :state].astype(jnp.float32)
    c_rows = bc[:, state:].astype(jnp.float32)
    tail_weight = jnp.exp(running[-1:, :] - running) * step_sizes
    weighted = channels.astype(jnp.float32).reshape(length, heads, width) * tail_weight[:, :, None]
    own_state = jnp.einsum("thp,tn->hpn", weighted, b_rows, precision=HIGH)
    scaled_grad = upstream.reshape(length, heads, width) * jnp.exp(running)[:, :, None]
    back_term = jnp.einsum("thp,tn->hpn", scaled_grad, c_rows, precision=HIGH)
    incoming, outgoing_grad = exchange(running[-1], own_state, back_term)

    def whole_block(bc_in, x_in, alog_in):
        return block_forward(bc_in, x_in, step_raw, alog_in, incoming)

    _, pull_all = jax.vjp(whole_block, bc, channels, a_log)
    d_bc, d_x, d_rate = pull_all((upstream, outgoing_grad))
    d_weight = lax.dot_general(
        tokens_here, d_bc, (((0,), (0,)), ((), ())), preferred_element_type=jnp.float32
    )
    axes = ("chain", "dp")
    total = lax.axis_size(axes)
    rows, cols = d_weight.shape
    chunk = rows // total
    rate_rows = jnp.zeros((8, cols), jnp.float32).at[0, :heads].set(d_rate)
    parcel = jnp.concatenate(
        [d_weight.reshape(total, chunk, cols), jnp.broadcast_to(rate_rows[None], (total, 8, cols))], axis=1
    )
    pieces = lax.all_to_all(parcel, axes, 0, 0, tiled=True)
    mine_sum = jnp.sum(pieces, axis=0)
    spread = jnp.broadcast_to(mine_sum[None], (total, chunk + 8, cols))
    gathered = lax.all_to_all(spread, axes, 0, 0, tiled=True)
    d_wbc = gathered[:, :chunk].reshape(rows, cols)
    d_alog = gathered[0, chunk, :heads]
    return (d_x[None], d_wbc, d_alog)


def solution(mesh):
    return jax.shard_map(
        per_device,
        mesh=mesh,
        in_specs=(
            P("dp", "chain", None),
            P(),
            P("dp", "chain", None),
            P("dp", "chain", None),
            P(),
            P("dp", "chain", None),
        ),
        out_specs=(P("dp", "chain", None), P(), P()),
        check_vma=False,
    )
```

```python
import jax
import jax.numpy as jnp
from jax import lax
from jax.sharding import PartitionSpec as P

GROUP = 128


HIGH = lax.Precision.HIGHEST


def exchange(log_total, own_state, back_term):
    count, mine = (lax.axis_size("chain"), lax.axis_index("chain"))
    heads, width, state = own_state.shape
    per = heads // count
    marks = jnp.broadcast_to(log_total[:, None, None], (heads, 8, state))
    both = jnp.stack(
        [jnp.concatenate([own_state, marks], axis=1), jnp.concatenate([back_term, marks], axis=1)], axis=1
    )
    sent = lax.all_to_all(both, "chain", 0, 0, tiled=True).reshape(count, per, 2, width + 8, state)
    parts = sent[:, :, :, :width]
    mine_logs = sent[:, :, 0, width, 0]
    edge = jnp.cumsum(mine_logs, axis=0) - mine_logs
    after = edge + mine_logs
    pos = jnp.arange(count, dtype=jnp.int32)
    earlier = pos[None, :] < pos[:, None]
    fwd_w = jnp.exp(jnp.where(earlier[:, :, None], edge[:, None, :] - after[None, :, :], -jnp.inf))
    bwd_w = jnp.exp(jnp.where(earlier.T[:, :, None], edge[None, :, :] - after[:, None, :], -jnp.inf))
    inc = jnp.einsum("djh,jhpn->dhpn", fwd_w, parts[:, :, 0], precision=HIGH)
    out = jnp.einsum("djh,jhpn->dhpn", bwd_w, parts[:, :, 1], precision=HIGH)
    res = jnp.stack([inc, out], axis=2).reshape(count * per, 2, width, state)
    back = lax.all_to_all(res, "chain", 0, 0, tiled=True)
    return back[:, 0], back[:, 1]


def block_forward(bc, x, dt_raw, a_log, h_in):
    length = x.shape[0]
    heads = h_in.shape[0]
    width = h_in.shape[1]
    state = h_in.shape[2]
    step = jax.nn.softplus(dt_raw)
    logdec = -step * jnp.exp(a_log)[None, :]
    b_in = bc[:, :state].astype(jnp.float32)
    c_out = bc[:, state:].astype(jnp.float32)
    inputs = x.astype(jnp.float32).reshape(length, heads, width) * step[:, :, None]
    decays = jnp.transpose(logdec, (1, 0))
    rows = jnp.arange(length, dtype=jnp.int32)
    causal = rows[:, None] >= rows[None, :]
    cum = jnp.cumsum(decays, axis=1)
    diff = cum[:, :, None] - cum[:, None, :]
    weights = jnp.exp(jnp.where(causal[None, :, :], diff, -jnp.inf))
    scores = jnp.einsum("tn,sn->ts", c_out, b_in, precision=HIGH)
    mixing = weights * scores[None, :, :]
    y_intra = jnp.einsum("hts,shp->thp", mixing, inputs, precision=HIGH)
    ends = cum[:, -1]
    tail = jnp.transpose(jnp.exp(ends[:, None] - cum), (1, 0))
    fresh = jnp.einsum("shp,sn->hpn", inputs * tail[:, :, None], b_in, precision=HIGH)
    h_end = fresh + jnp.exp(ends)[:, None, None] * h_in
    y_inter = (
        jnp.einsum("tn,hpn->thp", c_out, h_in, precision=HIGH)
        * jnp.exp(jnp.transpose(cum, (1, 0)))[:, :, None]
    )
    return ((y_intra + y_inter).reshape(length, heads * width), h_end)


def per_device(hidden, w_bc, xs, dt_raw, a_log, d_out):
    tokens_here = hidden[0]
    channels = xs[0]
    step_raw = dt_raw[0]
    upstream = d_out[0].astype(jnp.float32)
    heads = a_log.shape[0]
    width = channels.shape[1] // heads
    state = w_bc.shape[1] // 2
    length = channels.shape[0]
    bc = jnp.dot(tokens_here, w_bc, preferred_element_type=jnp.float32).astype(jnp.bfloat16)
    step_sizes = jax.nn.softplus(step_raw)
    log_decay = -step_sizes * jnp.exp(a_log)[None, :]
    running = jnp.cumsum(log_decay, axis=0)
    b_rows = bc[:, :state].astype(jnp.float32)
    c_rows = bc[:, state:].astype(jnp.float32)
    tail_weight = jnp.exp(running[-1:, :] - running) * step_sizes
    weighted = channels.astype(jnp.float32).reshape(length, heads, width) * tail_weight[:, :, None]
    own_state = jnp.einsum("thp,tn->hpn", weighted, b_rows, precision=HIGH)
    scaled_grad = upstream.reshape(length, heads, width) * jnp.exp(running)[:, :, None]
    back_term = jnp.einsum("thp,tn->hpn", scaled_grad, c_rows, precision=HIGH)
    incoming, outgoing_grad = exchange(running[-1], own_state, back_term)

    def whole_block(bc_in, x_in, alog_in):
        return block_forward(bc_in, x_in, step_raw, alog_in, incoming)

    _, pull_all = jax.vjp(whole_block, bc, channels, a_log)
    d_bc, d_x, d_rate = pull_all((upstream, outgoing_grad))
    d_weight = lax.dot_general(
        tokens_here, d_bc, (((0,), (0,)), ((), ())), preferred_element_type=jnp.float32
    )
    axes = ("chain", "dp")
    total = lax.axis_size(axes)
    rows, cols = d_weight.shape
    chunk = rows // total
    rate_rows = jnp.zeros((8, cols), jnp.float32).at[0, :heads].set(d_rate)
    parcel = jnp.concatenate(
        [d_weight.reshape(total, chunk, cols), jnp.broadcast_to(rate_rows[None], (total, 8, cols))], axis=1
    )
    pieces = lax.all_to_all(parcel, axes, 0, 0, tiled=True)
    mine_sum = jnp.sum(pieces, axis=0)
    spread = jnp.broadcast_to(mine_sum[None, :chunk], (total, chunk, cols))
    d_wbc = lax.all_to_all(spread, axes, 0, 0, tiled=True).reshape(rows, cols)
    d_alog = mine_sum[chunk, :heads]
    return (d_x[None], d_wbc, d_alog)


def solution(mesh):
    return jax.shard_map(
        per_device,
        mesh=mesh,
        in_specs=(
            P("dp", "chain", None),
            P(),
            P("dp", "chain", None),
            P("dp", "chain", None),
            P(),
            P("dp", "chain", None),
        ),
        out_specs=(P("dp", "chain", None), P(), P()),
        check_vma=False,
    )
```

```python
import jax
import jax.numpy as jnp
from jax import lax
from jax.sharding import Mesh, PartitionSpec as P

GROUP = 128
CHAIN = ("cz", "core")


HIGH = lax.Precision.HIGHEST


def exchange(log_total, own_state, back_term):
    count = lax.axis_size(CHAIN)
    heads, width, state = own_state.shape
    per = heads // count
    marks = jnp.broadcast_to(log_total[:, None, None], (heads, 8, state))
    both = jnp.stack(
        [jnp.concatenate([own_state, marks], axis=1), jnp.concatenate([back_term, marks], axis=1)], axis=1
    )
    sent = lax.all_to_all(both, CHAIN, 0, 0, tiled=True).reshape(count, per, 2, width + 8, state)
    parts = sent[:, :, :, :width]
    mine_logs = sent[:, :, 0, width, 0]
    edge = jnp.cumsum(mine_logs, axis=0) - mine_logs
    after = edge + mine_logs
    pos = jnp.arange(count, dtype=jnp.int32)
    earlier = pos[None, :] < pos[:, None]
    fwd_w = jnp.exp(jnp.where(earlier[:, :, None], edge[:, None, :] - after[None, :, :], -jnp.inf))
    bwd_w = jnp.exp(jnp.where(earlier.T[:, :, None], edge[None, :, :] - after[:, None, :], -jnp.inf))
    inc = jnp.einsum("djh,jhpn->dhpn", fwd_w, parts[:, :, 0], precision=HIGH)
    out = jnp.einsum("djh,jhpn->dhpn", bwd_w, parts[:, :, 1], precision=HIGH)
    res = jnp.stack([inc, out], axis=2).reshape(count * per, 2, width, state)
    back = lax.all_to_all(res, CHAIN, 0, 0, tiled=True)
    return back[:, 0], back[:, 1]


def block_forward(bc, x, dt_raw, a_log, h_in):
    length = x.shape[0]
    heads = h_in.shape[0]
    width = h_in.shape[1]
    state = h_in.shape[2]
    step = jax.nn.softplus(dt_raw)
    logdec = -step * jnp.exp(a_log)[None, :]
    b_in = bc[:, :state].astype(jnp.float32)
    c_out = bc[:, state:].astype(jnp.float32)
    inputs = x.astype(jnp.float32).reshape(length, heads, width) * step[:, :, None]
    decays = jnp.transpose(logdec, (1, 0))
    rows = jnp.arange(length, dtype=jnp.int32)
    causal = rows[:, None] >= rows[None, :]
    cum = jnp.cumsum(decays, axis=1)
    diff = cum[:, :, None] - cum[:, None, :]
    weights = jnp.exp(jnp.where(causal[None, :, :], diff, -jnp.inf))
    scores = jnp.einsum("tn,sn->ts", c_out, b_in, precision=HIGH)
    mixing = weights * scores[None, :, :]
    y_intra = jnp.einsum("hts,shp->thp", mixing, inputs, precision=HIGH)
    ends = cum[:, -1]
    tail = jnp.transpose(jnp.exp(ends[:, None] - cum), (1, 0))
    fresh = jnp.einsum("shp,sn->hpn", inputs * tail[:, :, None], b_in, precision=HIGH)
    h_end = fresh + jnp.exp(ends)[:, None, None] * h_in
    y_inter = (
        jnp.einsum("tn,hpn->thp", c_out, h_in, precision=HIGH)
        * jnp.exp(jnp.transpose(cum, (1, 0)))[:, :, None]
    )
    return ((y_intra + y_inter).reshape(length, heads * width), h_end)


def per_device(hidden, w_bc, xs, dt_raw, a_log, d_out):
    tokens_here = hidden[0]
    channels = xs[0]
    step_raw = dt_raw[0]
    upstream = d_out[0].astype(jnp.float32)
    heads = a_log.shape[0]
    width = channels.shape[1] // heads
    state = w_bc.shape[1] // 2
    length = channels.shape[0]
    bc = jnp.dot(tokens_here, w_bc, preferred_element_type=jnp.float32).astype(jnp.bfloat16)
    step_sizes = jax.nn.softplus(step_raw)
    log_decay = -step_sizes * jnp.exp(a_log)[None, :]
    running = jnp.cumsum(log_decay, axis=0)
    b_rows = bc[:, :state].astype(jnp.float32)
    c_rows = bc[:, state:].astype(jnp.float32)
    tail_weight = jnp.exp(running[-1:, :] - running) * step_sizes
    weighted = channels.astype(jnp.float32).reshape(length, heads, width) * tail_weight[:, :, None]
    own_state = jnp.einsum("thp,tn->hpn", weighted, b_rows, precision=HIGH)
    scaled_grad = upstream.reshape(length, heads, width) * jnp.exp(running)[:, :, None]
    back_term = jnp.einsum("thp,tn->hpn", scaled_grad, c_rows, precision=HIGH)
    incoming, outgoing_grad = exchange(running[-1], own_state, back_term)

    def whole_block(bc_in, x_in, alog_in):
        return block_forward(bc_in, x_in, step_raw, alog_in, incoming)

    _, pull_all = jax.vjp(whole_block, bc, channels, a_log)
    d_bc, d_x, d_rate = pull_all((upstream, outgoing_grad))
    d_weight = lax.dot_general(
        tokens_here, d_bc, (((0,), (0,)), ((), ())), preferred_element_type=jnp.float32
    )
    rows, cols = d_weight.shape
    half = rows // 2
    core = lax.axis_index("core")
    rate_rows = jnp.zeros((8, cols), jnp.float32).at[0, :heads].set(d_rate)
    halves = d_weight.reshape(2, half, cols)
    keep = jnp.concatenate([lax.dynamic_index_in_dim(halves, core, 0, keepdims=False), rate_rows], axis=0)
    give = jnp.concatenate([lax.dynamic_index_in_dim(halves, 1 - core, 0, keepdims=False), rate_rows], axis=0)
    paired = keep + lax.ppermute(give, "core", [(0, 1), (1, 0)])
    axes = ("cz", "dp")
    total = lax.axis_size(axes)
    chunk = half // total
    parcel = jnp.concatenate(
        [paired[:half].reshape(total, chunk, cols), jnp.broadcast_to(paired[None, half:], (total, 8, cols))], axis=1
    )
    pieces = lax.all_to_all(parcel, axes, 0, 0, tiled=True)
    mine_sum = jnp.sum(pieces, axis=0)
    spread = jnp.broadcast_to(mine_sum[None, :chunk], (total, chunk, cols))
    own_half = lax.all_to_all(spread, axes, 0, 0, tiled=True).reshape(half, cols)
    other_half = lax.ppermute(own_half, "core", [(0, 1), (1, 0)])
    first = core == 0
    d_wbc = jnp.concatenate(
        [jnp.where(first, own_half, other_half), jnp.where(first, other_half, own_half)], axis=0
    )
    d_alog = mine_sum[chunk, :heads]
    return (d_x[None], d_wbc, d_alog)


def solution(mesh):
    rows, dp = mesh.devices.shape
    split = Mesh(mesh.devices.reshape(rows // 2, 2, dp), ("cz", "core", "dp"))
    blocks = P("dp", CHAIN, None)
    return jax.shard_map(
        per_device,
        mesh=split,
        in_specs=(blocks, P(), blocks, blocks, P(), blocks),
        out_specs=(blocks, P(), P()),
        check_vma=False,
    )
```

```python
import jax
import jax.numpy as jnp
from jax import lax
from jax.sharding import Mesh, PartitionSpec as P

GROUP = 128
CHAIN = ("cz", "core")


HIGH = lax.Precision.HIGHEST


def exchange(log_total, own_state, back_term):
    count = lax.axis_size(CHAIN)
    heads, width, state = own_state.shape
    per = heads // count
    marks = jnp.broadcast_to(log_total[:, None, None], (heads, 8, state))
    both = jnp.stack(
        [jnp.concatenate([own_state, marks], axis=1), jnp.concatenate([back_term, marks], axis=1)], axis=1
    )
    sent = lax.all_to_all(both, CHAIN, 0, 0, tiled=True).reshape(count, per, 2, width + 8, state)
    parts = sent[:, :, :, :width]
    mine_logs = sent[:, :, 0, width, 0]
    edge = jnp.cumsum(mine_logs, axis=0) - mine_logs
    after = edge + mine_logs
    pos = jnp.arange(count, dtype=jnp.int32)
    earlier = pos[None, :] < pos[:, None]
    fwd_w = jnp.exp(jnp.where(earlier[:, :, None], edge[:, None, :] - after[None, :, :], -jnp.inf))
    bwd_w = jnp.exp(jnp.where(earlier.T[:, :, None], edge[None, :, :] - after[:, None, :], -jnp.inf))
    inc = jnp.einsum("djh,jhpn->dhpn", fwd_w, parts[:, :, 0], precision=HIGH)
    out = jnp.einsum("djh,jhpn->dhpn", bwd_w, parts[:, :, 1], precision=HIGH)
    res = jnp.stack([inc, out], axis=2).reshape(count * per, 2, width, state)
    back = lax.all_to_all(res, CHAIN, 0, 0, tiled=True)
    return back[:, 0], back[:, 1]


def block_forward(bc, x, dt_raw, a_log, h_in):
    length = x.shape[0]
    heads = h_in.shape[0]
    width = h_in.shape[1]
    state = h_in.shape[2]
    step = jax.nn.softplus(dt_raw)
    logdec = -step * jnp.exp(a_log)[None, :]
    b_in = bc[:, :state].astype(jnp.float32)
    c_out = bc[:, state:].astype(jnp.float32)
    inputs = x.astype(jnp.float32).reshape(length, heads, width) * step[:, :, None]
    decays = jnp.transpose(logdec, (1, 0))
    rows = jnp.arange(length, dtype=jnp.int32)
    causal = rows[:, None] >= rows[None, :]
    cum = jnp.cumsum(decays, axis=1)
    diff = cum[:, :, None] - cum[:, None, :]
    weights = jnp.exp(jnp.where(causal[None, :, :], diff, -jnp.inf))
    scores = jnp.einsum("tn,sn->ts", c_out, b_in, precision=HIGH)
    mixing = weights * scores[None, :, :]
    y_intra = jnp.einsum("hts,shp->thp", mixing, inputs, precision=HIGH)
    ends = cum[:, -1]
    tail = jnp.transpose(jnp.exp(ends[:, None] - cum), (1, 0))
    fresh = jnp.einsum("shp,sn->hpn", inputs * tail[:, :, None], b_in, precision=HIGH)
    h_end = fresh + jnp.exp(ends)[:, None, None] * h_in
    y_inter = (
        jnp.einsum("tn,hpn->thp", c_out, h_in, precision=HIGH)
        * jnp.exp(jnp.transpose(cum, (1, 0)))[:, :, None]
    )
    return ((y_intra + y_inter).reshape(length, heads * width), h_end)


def per_device(hidden, w_bc, xs, dt_raw, a_log, d_out):
    tokens_here = hidden[0]
    channels = xs[0]
    step_raw = dt_raw[0]
    upstream = d_out[0].astype(jnp.float32)
    heads = a_log.shape[0]
    width = channels.shape[1] // heads
    state = w_bc.shape[1] // 2
    length = channels.shape[0]
    bc = jnp.dot(tokens_here, w_bc, preferred_element_type=jnp.float32).astype(jnp.bfloat16)
    step_sizes = jax.nn.softplus(step_raw)
    log_decay = -step_sizes * jnp.exp(a_log)[None, :]
    running = jnp.cumsum(log_decay, axis=0)
    b_rows = bc[:, :state].astype(jnp.float32)
    c_rows = bc[:, state:].astype(jnp.float32)
    tail_weight = jnp.exp(running[-1:, :] - running) * step_sizes
    weighted = channels.astype(jnp.float32).reshape(length, heads, width) * tail_weight[:, :, None]
    own_state = jnp.einsum("thp,tn->hpn", weighted, b_rows, precision=HIGH)
    scaled_grad = upstream.reshape(length, heads, width) * jnp.exp(running)[:, :, None]
    back_term = jnp.einsum("thp,tn->hpn", scaled_grad, c_rows, precision=HIGH)
    incoming, outgoing_grad = exchange(running[-1], own_state, back_term)

    def whole_block(bc_in, x_in, alog_in):
        return block_forward(bc_in, x_in, step_raw, alog_in, incoming)

    _, pull_all = jax.vjp(whole_block, bc, channels, a_log)
    d_bc, d_x, d_rate = pull_all((upstream, outgoing_grad))
    rows, cols = tokens_here.shape[1], d_bc.shape[1]
    half = rows // 2
    first = lax.axis_index("core") == 0
    top, bottom = tokens_here[:, :half], tokens_here[:, half:]
    dims = (((0,), (0,)), ((), ()))
    keep = lax.dot_general(jnp.where(first, top, bottom), d_bc, dims, preferred_element_type=jnp.float32)
    give = lax.dot_general(jnp.where(first, bottom, top), d_bc, dims, preferred_element_type=jnp.float32)
    rate_rows = jnp.zeros((8, cols), jnp.float32).at[0, :heads].set(d_rate)
    swap = [(0, 1), (1, 0)]
    paired = keep + lax.ppermute(give, "core", swap)
    rate_pair = rate_rows + lax.ppermute(rate_rows, "core", swap)
    axes = ("cz", "dp")
    total = lax.axis_size(axes)
    chunk = half // total
    parcel = jnp.concatenate(
        [paired.reshape(total, chunk, cols), jnp.broadcast_to(rate_pair[None], (total, 8, cols))], axis=1
    )
    pieces = lax.all_to_all(parcel, axes, 0, 0, tiled=True)
    mine_sum = jnp.sum(pieces, axis=0)
    spread = jnp.broadcast_to(mine_sum[None, :chunk], (total, chunk, cols))
    own_half = lax.all_to_all(spread, axes, 0, 0, tiled=True).reshape(half, cols)
    other_half = lax.ppermute(own_half, "core", swap)
    d_wbc = jnp.concatenate(
        [jnp.where(first, own_half, other_half), jnp.where(first, other_half, own_half)], axis=0
    )
    d_alog = mine_sum[chunk, :heads]
    return (d_x[None], d_wbc, d_alog)


def solution(mesh):
    rows, dp = mesh.devices.shape
    split = Mesh(mesh.devices.reshape(rows // 2, 2, dp), ("cz", "core", "dp"))
    blocks = P("dp", CHAIN, None)
    return jax.shard_map(
        per_device,
        mesh=split,
        in_specs=(blocks, P(), blocks, blocks, P(), blocks),
        out_specs=(blocks, P(), P()),
        check_vma=False,
    )
```

```python
import jax
import jax.numpy as jnp
from jax import lax
from jax.sharding import Mesh, PartitionSpec as P

GROUP = 128
CHAIN = ("cz", "core")


HIGH = lax.Precision.HIGHEST


def exchange(log_total, own_state, back_term):
    heads, width, state = own_state.shape
    first = lax.axis_index("core") == 0
    swap = [(0, 1), (1, 0)]

    def marked(value, logs):
        return jnp.concatenate([value, jnp.broadcast_to(logs[:, None, None], (heads, 8, state))], axis=1)

    got = lax.ppermute(marked(jnp.where(first, own_state, back_term), log_total), "core", swap)
    partner = got[:, :width]
    partner_log = got[:, width, 0]
    pair_log = log_total + partner_log
    mine = jnp.where(first, back_term, own_state)
    combined = mine + jnp.exp(log_total)[:, None, None] * partner
    count = lax.axis_size("cz")
    per = heads // count
    sent = lax.all_to_all(marked(combined, pair_log), "cz", 0, 0, tiled=True).reshape(count, per, width + 8, state)
    parts = sent[:, :, :width]
    chip_logs = sent[:, :, width, 0]
    edge = jnp.cumsum(chip_logs, axis=0) - chip_logs
    after = edge + chip_logs
    pos = jnp.arange(count, dtype=jnp.int32)
    earlier = pos[None, :] < pos[:, None]
    fwd_w = jnp.exp(jnp.where(earlier[:, :, None], edge[:, None, :] - after[None, :, :], -jnp.inf))
    bwd_w = jnp.exp(jnp.where(earlier.T[:, :, None], edge[None, :, :] - after[:, None, :], -jnp.inf))
    weight = jnp.where(first, bwd_w, fwd_w)
    res = jnp.einsum("djh,jhpn->dhpn", weight, parts, precision=HIGH).reshape(count * per, width, state)
    back = lax.all_to_all(res, "cz", 0, 0, tiled=True)
    other = lax.ppermute(back, "core", swap)
    fixed = jnp.exp(partner_log)[:, None, None] * back + partner
    return jnp.where(first, other, fixed), jnp.where(first, fixed, other)


def block_forward(bc, x, dt_raw, a_log, h_in):
    length = x.shape[0]
    heads = h_in.shape[0]
    width = h_in.shape[1]
    state = h_in.shape[2]
    step = jax.nn.softplus(dt_raw)
    logdec = -step * jnp.exp(a_log)[None, :]
    b_in = bc[:, :state].astype(jnp.float32)
    c_out = bc[:, state:].astype(jnp.float32)
    inputs = x.astype(jnp.float32).reshape(length, heads, width) * step[:, :, None]
    decays = jnp.transpose(logdec, (1, 0))
    rows = jnp.arange(length, dtype=jnp.int32)
    causal = rows[:, None] >= rows[None, :]
    cum = jnp.cumsum(decays, axis=1)
    diff = cum[:, :, None] - cum[:, None, :]
    weights = jnp.exp(jnp.where(causal[None, :, :], diff, -jnp.inf))
    scores = jnp.einsum("tn,sn->ts", c_out, b_in, precision=HIGH)
    mixing = weights * scores[None, :, :]
    y_intra = jnp.einsum("hts,shp->thp", mixing, inputs, precision=HIGH)
    ends = cum[:, -1]
    tail = jnp.transpose(jnp.exp(ends[:, None] - cum), (1, 0))
    fresh = jnp.einsum("shp,sn->hpn", inputs * tail[:, :, None], b_in, precision=HIGH)
    h_end = fresh + jnp.exp(ends)[:, None, None] * h_in
    y_inter = (
        jnp.einsum("tn,hpn->thp", c_out, h_in, precision=HIGH)
        * jnp.exp(jnp.transpose(cum, (1, 0)))[:, :, None]
    )
    return ((y_intra + y_inter).reshape(length, heads * width), h_end)


def per_device(hidden, w_bc, xs, dt_raw, a_log, d_out):
    tokens_here = hidden[0]
    channels = xs[0]
    step_raw = dt_raw[0]
    upstream = d_out[0].astype(jnp.float32)
    heads = a_log.shape[0]
    width = channels.shape[1] // heads
    state = w_bc.shape[1] // 2
    length = channels.shape[0]
    bc = jnp.dot(tokens_here, w_bc, preferred_element_type=jnp.float32).astype(jnp.bfloat16)
    step_sizes = jax.nn.softplus(step_raw)
    log_decay = -step_sizes * jnp.exp(a_log)[None, :]
    running = jnp.cumsum(log_decay, axis=0)
    b_rows = bc[:, :state].astype(jnp.float32)
    c_rows = bc[:, state:].astype(jnp.float32)
    tail_weight = jnp.exp(running[-1:, :] - running) * step_sizes
    weighted = channels.astype(jnp.float32).reshape(length, heads, width) * tail_weight[:, :, None]
    own_state = jnp.einsum("thp,tn->hpn", weighted, b_rows, precision=HIGH)
    scaled_grad = upstream.reshape(length, heads, width) * jnp.exp(running)[:, :, None]
    back_term = jnp.einsum("thp,tn->hpn", scaled_grad, c_rows, precision=HIGH)
    incoming, outgoing_grad = exchange(running[-1], own_state, back_term)

    def whole_block(bc_in, x_in, alog_in):
        return block_forward(bc_in, x_in, step_raw, alog_in, incoming)

    _, pull_all = jax.vjp(whole_block, bc, channels, a_log)
    d_bc, d_x, d_rate = pull_all((upstream, outgoing_grad))
    rows, cols = tokens_here.shape[1], d_bc.shape[1]
    half = rows // 2
    first = lax.axis_index("core") == 0
    top, bottom = tokens_here[:, :half], tokens_here[:, half:]
    dims = (((0,), (0,)), ((), ()))
    keep = lax.dot_general(jnp.where(first, top, bottom), d_bc, dims, preferred_element_type=jnp.float32)
    give = lax.dot_general(jnp.where(first, bottom, top), d_bc, dims, preferred_element_type=jnp.float32)
    rate_rows = jnp.zeros((8, cols), jnp.float32).at[0, :heads].set(d_rate)
    swap = [(0, 1), (1, 0)]
    paired = keep + lax.ppermute(give, "core", swap)
    rate_pair = rate_rows + lax.ppermute(rate_rows, "core", swap)
    axes = ("cz", "dp")
    total = lax.axis_size(axes)
    chunk = half // total
    parcel = jnp.concatenate(
        [paired.reshape(total, chunk, cols), jnp.broadcast_to(rate_pair[None], (total, 8, cols))], axis=1
    )
    pieces = lax.all_to_all(parcel, axes, 0, 0, tiled=True)
    mine_sum = jnp.sum(pieces, axis=0)
    spread = jnp.broadcast_to(mine_sum[None, :chunk], (total, chunk, cols))
    own_half = lax.all_to_all(spread, axes, 0, 0, tiled=True).reshape(half, cols)
    other_half = lax.ppermute(own_half, "core", swap)
    d_wbc = jnp.concatenate(
        [jnp.where(first, own_half, other_half), jnp.where(first, other_half, own_half)], axis=0
    )
    d_alog = mine_sum[chunk, :heads]
    return (d_x[None], d_wbc, d_alog)


def solution(mesh):
    rows, dp = mesh.devices.shape
    split = Mesh(mesh.devices.reshape(rows // 2, 2, dp), ("cz", "core", "dp"))
    blocks = P("dp", CHAIN, None)
    return jax.shard_map(
        per_device,
        mesh=split,
        in_specs=(blocks, P(), blocks, blocks, P(), blocks),
        out_specs=(blocks, P(), P()),
        check_vma=False,
    )
```

```python
import jax
import jax.numpy as jnp
from jax import lax
from jax.sharding import Mesh, PartitionSpec as P

GROUP = 128
CHAIN = ("cz", "core")


HIGH = lax.Precision.HIGHEST


def exchange(log_total, own_state, back_term):
    heads, width, state = own_state.shape
    first = lax.axis_index("core") == 0
    swap = [(0, 1), (1, 0)]

    def marked(value, logs):
        return jnp.concatenate([value, jnp.broadcast_to(logs[:, None, None], (heads, 8, state))], axis=1)

    got = lax.ppermute(marked(jnp.where(first, own_state, back_term), log_total), "core", swap)
    partner = got[:, :width]
    partner_log = got[:, width, 0]
    pair_log = log_total + partner_log
    mine = jnp.where(first, back_term, own_state)
    combined = mine + jnp.exp(log_total)[:, None, None] * partner
    count = lax.axis_size("cz")
    per = heads // count
    sent = lax.all_to_all(marked(combined, pair_log), "cz", 0, 0, tiled=True).reshape(count, per, width + 8, state)
    parts = sent[:, :, :width]
    chip_logs = sent[:, :, width, 0]
    edge = jnp.cumsum(chip_logs, axis=0) - chip_logs
    after = edge + chip_logs
    pos = jnp.arange(count, dtype=jnp.int32)
    earlier = pos[None, :] < pos[:, None]
    fwd_w = jnp.exp(jnp.where(earlier[:, :, None], edge[:, None, :] - after[None, :, :], -jnp.inf))
    bwd_w = jnp.exp(jnp.where(earlier.T[:, :, None], edge[None, :, :] - after[:, None, :], -jnp.inf))
    weight = jnp.where(first, bwd_w, fwd_w)
    res = jnp.einsum("djh,jhpn->dhpn", weight, parts, precision=HIGH).reshape(count * per, width, state)
    back = lax.all_to_all(res, "cz", 0, 0, tiled=True)
    other = lax.ppermute(back, "core", swap)
    fixed = jnp.exp(partner_log)[:, None, None] * back + partner
    return jnp.where(first, other, fixed), jnp.where(first, fixed, other)


def block_forward(bc, x, dt_raw, a_log, h_in):
    length = x.shape[0]
    heads = h_in.shape[0]
    width = h_in.shape[1]
    state = h_in.shape[2]
    step = jax.nn.softplus(dt_raw)
    logdec = -step * jnp.exp(a_log)[None, :]
    b_in = bc[:, :state].astype(jnp.float32)
    c_out = bc[:, state:].astype(jnp.float32)
    inputs = x.astype(jnp.float32).reshape(length, heads, width) * step[:, :, None]
    decays = jnp.transpose(logdec, (1, 0))
    rows = jnp.arange(length, dtype=jnp.int32)
    causal = rows[:, None] >= rows[None, :]
    cum = jnp.cumsum(decays, axis=1)
    diff = cum[:, :, None] - cum[:, None, :]
    weights = jnp.exp(jnp.where(causal[None, :, :], diff, -jnp.inf))
    scores = jnp.einsum("tn,sn->ts", c_out, b_in, precision=HIGH)
    mixing = weights * scores[None, :, :]
    y_intra = jnp.einsum("hts,shp->thp", mixing, inputs, precision=HIGH)
    ends = cum[:, -1]
    tail = jnp.transpose(jnp.exp(ends[:, None] - cum), (1, 0))
    fresh = jnp.einsum("shp,sn->hpn", inputs * tail[:, :, None], b_in, precision=HIGH)
    h_end = fresh + jnp.exp(ends)[:, None, None] * h_in
    y_inter = (
        jnp.einsum("tn,hpn->thp", c_out, h_in, precision=HIGH)
        * jnp.exp(jnp.transpose(cum, (1, 0)))[:, :, None]
    )
    return ((y_intra + y_inter).reshape(length, heads * width), h_end)


def per_device(hidden, w_bc, xs, dt_raw, a_log, d_out):
    tokens_here = hidden[0]
    channels = xs[0]
    step_raw = dt_raw[0]
    upstream = d_out[0].astype(jnp.float32)
    heads = a_log.shape[0]
    width = channels.shape[1] // heads
    state = w_bc.shape[1] // 2
    length = channels.shape[0]
    bc = jnp.dot(tokens_here, w_bc, preferred_element_type=jnp.float32).astype(jnp.bfloat16)
    step_sizes = jax.nn.softplus(step_raw)
    log_decay = -step_sizes * jnp.exp(a_log)[None, :]
    running = jnp.cumsum(log_decay, axis=0)
    b_rows = bc[:, :state].astype(jnp.float32)
    c_rows = bc[:, state:].astype(jnp.float32)
    tail_weight = jnp.exp(running[-1:, :] - running) * step_sizes
    weighted = channels.astype(jnp.float32).reshape(length, heads, width) * tail_weight[:, :, None]
    own_state = jnp.einsum("thp,tn->hpn", weighted, b_rows, precision=HIGH)
    scaled_grad = upstream.reshape(length, heads, width) * jnp.exp(running)[:, :, None]
    back_term = jnp.einsum("thp,tn->hpn", scaled_grad, c_rows, precision=HIGH)
    incoming, outgoing_grad = exchange(running[-1], own_state, back_term)

    def whole_block(bc_in, x_in, alog_in):
        return block_forward(bc_in, x_in, step_raw, alog_in, incoming)

    _, pull_all = jax.vjp(whole_block, bc, channels, a_log)
    d_bc, d_x, d_rate = pull_all((upstream, outgoing_grad))
    rows, cols = tokens_here.shape[1], d_bc.shape[1]
    half = rows // 2
    first = lax.axis_index("core") == 0
    top, bottom = tokens_here[:, :half], tokens_here[:, half:]
    dims = (((0,), (0,)), ((), ()))
    keep = lax.dot_general(jnp.where(first, top, bottom), d_bc, dims, preferred_element_type=jnp.float32)
    give = lax.dot_general(jnp.where(first, bottom, top), d_bc, dims, preferred_element_type=jnp.float32)
    rate_rows = jnp.zeros((8, cols), jnp.float32).at[0, :heads].set(d_rate)
    swap = [(0, 1), (1, 0)]
    paired = keep + lax.ppermute(give, "core", swap)
    rate_pair = rate_rows + lax.ppermute(rate_rows, "core", swap)
    level = []
    block = paired
    extra = rate_pair
    for axis in ("dp", "cz"):
        total = lax.axis_size(axis)
        chunk = block.shape[0] // total
        parcel = jnp.concatenate(
            [block.reshape(total, chunk, cols), jnp.broadcast_to(extra[None], (total, 8, cols))], axis=1
        )
        summed = jnp.sum(lax.all_to_all(parcel, axis, 0, 0, tiled=True), axis=0)
        level.append((axis, total, chunk))
        block, extra = summed[:chunk], summed[chunk:]
    d_alog = extra[0, :heads]
    for axis, total, chunk in level[::-1]:
        block = lax.all_to_all(jnp.broadcast_to(block[None], (total, chunk, cols)), axis, 0, 0, tiled=True)
        block = block.reshape(total * chunk, cols)
    own_half = block
    other_half = lax.ppermute(own_half, "core", swap)
    d_wbc = jnp.concatenate(
        [jnp.where(first, own_half, other_half), jnp.where(first, other_half, own_half)], axis=0
    )
    return (d_x[None], d_wbc, d_alog)


def solution(mesh):
    rows, dp = mesh.devices.shape
    split = Mesh(mesh.devices.reshape(rows // 2, 2, dp), ("cz", "core", "dp"))
    blocks = P("dp", CHAIN, None)
    return jax.shard_map(
        per_device,
        mesh=split,
        in_specs=(blocks, P(), blocks, blocks, P(), blocks),
        out_specs=(blocks, P(), P()),
        check_vma=False,
    )
```

```python
import jax
import jax.numpy as jnp
from jax import lax
from jax.sharding import Mesh, PartitionSpec as P

GROUP = 128
CHAIN = ("cz", "core")


HIGH = lax.Precision.HIGHEST


def shuffle(value, axis):
    count, mine = (lax.axis_size(axis), lax.axis_index(axis))
    chunks = value.reshape(count, value.shape[0] // count, *value.shape[1:])
    result = lax.dynamic_update_index_in_dim(
        jnp.zeros_like(chunks), lax.dynamic_index_in_dim(chunks, mine, 0, keepdims=False), mine, 0
    )
    for shift in range(1, count):
        piece = lax.dynamic_index_in_dim(chunks, (mine + shift) % count, 0, keepdims=False)
        got = lax.ppermute(piece, axis, [(i, (i + shift) % count) for i in range(count)])
        result = lax.dynamic_update_index_in_dim(result, got, (mine + count - shift) % count, 0)
    return result.reshape(value.shape)


def exchange(log_total, own_state, back_term):
    heads, width, state = own_state.shape
    first = lax.axis_index("core") == 0
    swap = [(0, 1), (1, 0)]

    def marked(value, logs):
        return jnp.concatenate([value, jnp.broadcast_to(logs[:, None, None], (heads, 8, state))], axis=1)

    got = lax.ppermute(marked(jnp.where(first, own_state, back_term), log_total), "core", swap)
    partner = got[:, :width]
    partner_log = got[:, width, 0]
    pair_log = log_total + partner_log
    mine = jnp.where(first, back_term, own_state)
    combined = mine + jnp.exp(log_total)[:, None, None] * partner
    count = lax.axis_size("cz")
    per = heads // count
    sent = shuffle(marked(combined, pair_log), "cz").reshape(count, per, width + 8, state)
    parts = sent[:, :, :width]
    chip_logs = sent[:, :, width, 0]
    edge = jnp.cumsum(chip_logs, axis=0) - chip_logs
    after = edge + chip_logs
    pos = jnp.arange(count, dtype=jnp.int32)
    earlier = pos[None, :] < pos[:, None]
    fwd_w = jnp.exp(jnp.where(earlier[:, :, None], edge[:, None, :] - after[None, :, :], -jnp.inf))
    bwd_w = jnp.exp(jnp.where(earlier.T[:, :, None], edge[None, :, :] - after[:, None, :], -jnp.inf))
    weight = jnp.where(first, bwd_w, fwd_w)
    res = jnp.einsum("djh,jhpn->dhpn", weight, parts, precision=HIGH).reshape(count * per, width, state)
    back = shuffle(res, "cz")
    other = lax.ppermute(back, "core", swap)
    fixed = jnp.exp(partner_log)[:, None, None] * back + partner
    return jnp.where(first, other, fixed), jnp.where(first, fixed, other)


def block_forward(bc, x, dt_raw, a_log, h_in):
    length = x.shape[0]
    heads = h_in.shape[0]
    width = h_in.shape[1]
    state = h_in.shape[2]
    step = jax.nn.softplus(dt_raw)
    logdec = -step * jnp.exp(a_log)[None, :]
    b_in = bc[:, :state].astype(jnp.float32)
    c_out = bc[:, state:].astype(jnp.float32)
    inputs = x.astype(jnp.float32).reshape(length, heads, width) * step[:, :, None]
    decays = jnp.transpose(logdec, (1, 0))
    rows = jnp.arange(length, dtype=jnp.int32)
    causal = rows[:, None] >= rows[None, :]
    cum = jnp.cumsum(decays, axis=1)
    diff = cum[:, :, None] - cum[:, None, :]
    weights = jnp.exp(jnp.where(causal[None, :, :], diff, -jnp.inf))
    scores = jnp.einsum("tn,sn->ts", c_out, b_in, precision=HIGH)
    mixing = weights * scores[None, :, :]
    y_intra = jnp.einsum("hts,shp->thp", mixing, inputs, precision=HIGH)
    ends = cum[:, -1]
    tail = jnp.transpose(jnp.exp(ends[:, None] - cum), (1, 0))
    fresh = jnp.einsum("shp,sn->hpn", inputs * tail[:, :, None], b_in, precision=HIGH)
    h_end = fresh + jnp.exp(ends)[:, None, None] * h_in
    y_inter = (
        jnp.einsum("tn,hpn->thp", c_out, h_in, precision=HIGH)
        * jnp.exp(jnp.transpose(cum, (1, 0)))[:, :, None]
    )
    return ((y_intra + y_inter).reshape(length, heads * width), h_end)


def per_device(hidden, w_bc, xs, dt_raw, a_log, d_out):
    tokens_here = hidden[0]
    channels = xs[0]
    step_raw = dt_raw[0]
    upstream = d_out[0].astype(jnp.float32)
    heads = a_log.shape[0]
    width = channels.shape[1] // heads
    state = w_bc.shape[1] // 2
    length = channels.shape[0]
    bc = jnp.dot(tokens_here, w_bc, preferred_element_type=jnp.float32).astype(jnp.bfloat16)
    step_sizes = jax.nn.softplus(step_raw)
    log_decay = -step_sizes * jnp.exp(a_log)[None, :]
    running = jnp.cumsum(log_decay, axis=0)
    b_rows = bc[:, :state].astype(jnp.float32)
    c_rows = bc[:, state:].astype(jnp.float32)
    tail_weight = jnp.exp(running[-1:, :] - running) * step_sizes
    weighted = channels.astype(jnp.float32).reshape(length, heads, width) * tail_weight[:, :, None]
    own_state = jnp.einsum("thp,tn->hpn", weighted, b_rows, precision=HIGH)
    scaled_grad = upstream.reshape(length, heads, width) * jnp.exp(running)[:, :, None]
    back_term = jnp.einsum("thp,tn->hpn", scaled_grad, c_rows, precision=HIGH)
    incoming, outgoing_grad = exchange(running[-1], own_state, back_term)

    def whole_block(bc_in, x_in, alog_in):
        return block_forward(bc_in, x_in, step_raw, alog_in, incoming)

    _, pull_all = jax.vjp(whole_block, bc, channels, a_log)
    d_bc, d_x, d_rate = pull_all((upstream, outgoing_grad))
    rows, cols = tokens_here.shape[1], d_bc.shape[1]
    half = rows // 2
    first = lax.axis_index("core") == 0
    top, bottom = tokens_here[:, :half], tokens_here[:, half:]
    dims = (((0,), (0,)), ((), ()))
    keep = lax.dot_general(jnp.where(first, top, bottom), d_bc, dims, preferred_element_type=jnp.float32)
    give = lax.dot_general(jnp.where(first, bottom, top), d_bc, dims, preferred_element_type=jnp.float32)
    rate_rows = jnp.zeros((8, cols), jnp.float32).at[0, :heads].set(d_rate)
    swap = [(0, 1), (1, 0)]
    paired = keep + lax.ppermute(give, "core", swap)
    rate_pair = rate_rows + lax.ppermute(rate_rows, "core", swap)
    axes = ("cz", "dp")
    total = lax.axis_size(axes)
    chunk = half // total
    parcel = jnp.concatenate(
        [paired.reshape(total, chunk, cols), jnp.broadcast_to(rate_pair[None], (total, 8, cols))], axis=1
    )
    pieces = lax.all_to_all(parcel, axes, 0, 0, tiled=True)
    mine_sum = jnp.sum(pieces, axis=0)
    spread = jnp.broadcast_to(mine_sum[None, :chunk], (total, chunk, cols))
    own_half = lax.all_to_all(spread, axes, 0, 0, tiled=True).reshape(half, cols)
    other_half = lax.ppermute(own_half, "core", swap)
    d_wbc = jnp.concatenate(
        [jnp.where(first, own_half, other_half), jnp.where(first, other_half, own_half)], axis=0
    )
    d_alog = mine_sum[chunk, :heads]
    return (d_x[None], d_wbc, d_alog)


def solution(mesh):
    rows, dp = mesh.devices.shape
    split = Mesh(mesh.devices.reshape(rows // 2, 2, dp), ("cz", "core", "dp"))
    blocks = P("dp", CHAIN, None)
    return jax.shard_map(
        per_device,
        mesh=split,
        in_specs=(blocks, P(), blocks, blocks, P(), blocks),
        out_specs=(blocks, P(), P()),
        check_vma=False,
    )
```

```python
import jax
import jax.numpy as jnp
from jax import lax
from jax.sharding import Mesh, PartitionSpec as P

GROUP = 128
CHAIN = ("cz", "core")


HIGH = lax.Precision.HIGH


def exchange(log_total, own_state, back_term):
    heads, width, state = own_state.shape
    first = lax.axis_index("core") == 0
    swap = [(0, 1), (1, 0)]

    def marked(value, logs):
        return jnp.concatenate([value, jnp.broadcast_to(logs[:, None, None], (heads, 8, state))], axis=1)

    got = lax.ppermute(marked(jnp.where(first, own_state, back_term), log_total), "core", swap)
    partner = got[:, :width]
    partner_log = got[:, width, 0]
    pair_log = log_total + partner_log
    mine = jnp.where(first, back_term, own_state)
    combined = mine + jnp.exp(log_total)[:, None, None] * partner
    count = lax.axis_size("cz")
    per = heads // count
    sent = lax.all_to_all(marked(combined, pair_log), "cz", 0, 0, tiled=True).reshape(count, per, width + 8, state)
    parts = sent[:, :, :width]
    chip_logs = sent[:, :, width, 0]
    edge = jnp.cumsum(chip_logs, axis=0) - chip_logs
    after = edge + chip_logs
    pos = jnp.arange(count, dtype=jnp.int32)
    earlier = pos[None, :] < pos[:, None]
    fwd_w = jnp.exp(jnp.where(earlier[:, :, None], edge[:, None, :] - after[None, :, :], -jnp.inf))
    bwd_w = jnp.exp(jnp.where(earlier.T[:, :, None], edge[None, :, :] - after[:, None, :], -jnp.inf))
    weight = jnp.where(first, bwd_w, fwd_w)
    res = jnp.einsum("djh,jhpn->dhpn", weight, parts, precision=HIGH).reshape(count * per, width, state)
    back = lax.all_to_all(res, "cz", 0, 0, tiled=True)
    other = lax.ppermute(back, "core", swap)
    fixed = jnp.exp(partner_log)[:, None, None] * back + partner
    return jnp.where(first, other, fixed), jnp.where(first, fixed, other)


def block_forward(bc, x, dt_raw, a_log, h_in):
    length = x.shape[0]
    heads = h_in.shape[0]
    width = h_in.shape[1]
    state = h_in.shape[2]
    step = jax.nn.softplus(dt_raw)
    logdec = -step * jnp.exp(a_log)[None, :]
    b_in = bc[:, :state].astype(jnp.float32)
    c_out = bc[:, state:].astype(jnp.float32)
    inputs = x.astype(jnp.float32).reshape(length, heads, width) * step[:, :, None]
    decays = jnp.transpose(logdec, (1, 0))
    rows = jnp.arange(length, dtype=jnp.int32)
    causal = rows[:, None] >= rows[None, :]
    cum = jnp.cumsum(decays, axis=1)
    diff = cum[:, :, None] - cum[:, None, :]
    weights = jnp.exp(jnp.where(causal[None, :, :], diff, -jnp.inf))
    scores = jnp.einsum("tn,sn->ts", c_out, b_in, precision=HIGH)
    mixing = weights * scores[None, :, :]
    y_intra = jnp.einsum("hts,shp->thp", mixing, inputs, precision=HIGH)
    ends = cum[:, -1]
    tail = jnp.transpose(jnp.exp(ends[:, None] - cum), (1, 0))
    fresh = jnp.einsum("shp,sn->hpn", inputs * tail[:, :, None], b_in, precision=HIGH)
    h_end = fresh + jnp.exp(ends)[:, None, None] * h_in
    y_inter = (
        jnp.einsum("tn,hpn->thp", c_out, h_in, precision=HIGH)
        * jnp.exp(jnp.transpose(cum, (1, 0)))[:, :, None]
    )
    return ((y_intra + y_inter).reshape(length, heads * width), h_end)


def per_device(hidden, w_bc, xs, dt_raw, a_log, d_out):
    tokens_here = hidden[0]
    channels = xs[0]
    step_raw = dt_raw[0]
    upstream = d_out[0].astype(jnp.float32)
    heads = a_log.shape[0]
    width = channels.shape[1] // heads
    state = w_bc.shape[1] // 2
    length = channels.shape[0]
    bc = jnp.dot(tokens_here, w_bc, preferred_element_type=jnp.float32).astype(jnp.bfloat16)
    step_sizes = jax.nn.softplus(step_raw)
    log_decay = -step_sizes * jnp.exp(a_log)[None, :]
    running = jnp.cumsum(log_decay, axis=0)
    b_rows = bc[:, :state].astype(jnp.float32)
    c_rows = bc[:, state:].astype(jnp.float32)
    tail_weight = jnp.exp(running[-1:, :] - running) * step_sizes
    weighted = channels.astype(jnp.float32).reshape(length, heads, width) * tail_weight[:, :, None]
    own_state = jnp.einsum("thp,tn->hpn", weighted, b_rows, precision=HIGH)
    scaled_grad = upstream.reshape(length, heads, width) * jnp.exp(running)[:, :, None]
    back_term = jnp.einsum("thp,tn->hpn", scaled_grad, c_rows, precision=HIGH)
    incoming, outgoing_grad = exchange(running[-1], own_state, back_term)

    def whole_block(bc_in, x_in, alog_in):
        return block_forward(bc_in, x_in, step_raw, alog_in, incoming)

    _, pull_all = jax.vjp(whole_block, bc, channels, a_log)
    d_bc, d_x, d_rate = pull_all((upstream, outgoing_grad))
    rows, cols = tokens_here.shape[1], d_bc.shape[1]
    half = rows // 2
    first = lax.axis_index("core") == 0
    top, bottom = tokens_here[:, :half], tokens_here[:, half:]
    dims = (((0,), (0,)), ((), ()))
    keep = lax.dot_general(jnp.where(first, top, bottom), d_bc, dims, preferred_element_type=jnp.float32)
    give = lax.dot_general(jnp.where(first, bottom, top), d_bc, dims, preferred_element_type=jnp.float32)
    rate_rows = jnp.zeros((8, cols), jnp.float32).at[0, :heads].set(d_rate)
    swap = [(0, 1), (1, 0)]
    paired = keep + lax.ppermute(give, "core", swap)
    rate_pair = rate_rows + lax.ppermute(rate_rows, "core", swap)
    axes = ("cz", "dp")
    total = lax.axis_size(axes)
    chunk = half // total
    parcel = jnp.concatenate(
        [paired.reshape(total, chunk, cols), jnp.broadcast_to(rate_pair[None], (total, 8, cols))], axis=1
    )
    pieces = lax.all_to_all(parcel, axes, 0, 0, tiled=True)
    mine_sum = jnp.sum(pieces, axis=0)
    spread = jnp.broadcast_to(mine_sum[None, :chunk], (total, chunk, cols))
    own_half = lax.all_to_all(spread, axes, 0, 0, tiled=True).reshape(half, cols)
    other_half = lax.ppermute(own_half, "core", swap)
    d_wbc = jnp.concatenate(
        [jnp.where(first, own_half, other_half), jnp.where(first, other_half, own_half)], axis=0
    )
    d_alog = mine_sum[chunk, :heads]
    return (d_x[None], d_wbc, d_alog)


def solution(mesh):
    rows, dp = mesh.devices.shape
    split = Mesh(mesh.devices.reshape(rows // 2, 2, dp), ("cz", "core", "dp"))
    blocks = P("dp", CHAIN, None)
    return jax.shard_map(
        per_device,
        mesh=split,
        in_specs=(blocks, P(), blocks, blocks, P(), blocks),
        out_specs=(blocks, P(), P()),
        check_vma=False,
    )
```

```python
import jax
import jax.numpy as jnp
from jax import lax
from jax.sharding import Mesh, PartitionSpec as P

GROUP = 128
CHAIN = ("cz", "core")


HIGH = lax.Precision.HIGH


def exchange(log_total, own_state, back_term):
    heads, width, state = own_state.shape
    first = lax.axis_index("core") == 0
    swap = [(0, 1), (1, 0)]

    def marked(value, logs):
        return jnp.concatenate([value, jnp.broadcast_to(logs[:, None, None], (heads, 8, state))], axis=1)

    got = lax.ppermute(marked(jnp.where(first, own_state, back_term), log_total), "core", swap)
    partner = got[:, :width]
    partner_log = got[:, width, 0]
    pair_log = log_total + partner_log
    mine = jnp.where(first, back_term, own_state)
    combined = mine + jnp.exp(log_total)[:, None, None] * partner
    count = lax.axis_size("cz")
    per = heads // count
    sent = lax.all_to_all(marked(combined, pair_log), "cz", 0, 0, tiled=True).reshape(count, per, width + 8, state)
    chip_logs = sent[:, :, width, 0]
    edge = jnp.cumsum(chip_logs, axis=0) - chip_logs
    after = edge + chip_logs
    pos = jnp.arange(count, dtype=jnp.int32)
    earlier = pos[None, :] < pos[:, None]
    fwd_w = jnp.exp(jnp.where(earlier[:, :, None], edge[:, None, :] - after[None, :, :], -jnp.inf))
    bwd_w = jnp.exp(jnp.where(earlier.T[:, :, None], edge[None, :, :] - after[:, None, :], -jnp.inf))
    weight = jnp.where(first, bwd_w, fwd_w)
    res = jnp.einsum("djh,jhpn->dhpn", weight, sent, precision=HIGH).reshape(count * per, width + 8, state)
    back = lax.all_to_all(res, "cz", 0, 0, tiled=True)
    other = lax.ppermute(back, "core", swap)[:, :width]
    fixed = jnp.exp(partner_log)[:, None, None] * back[:, :width] + partner
    return jnp.where(first, other, fixed), jnp.where(first, fixed, other)


def block_forward(bc, x, dt_raw, a_log, h_in):
    length = x.shape[0]
    heads = h_in.shape[0]
    width = h_in.shape[1]
    state = h_in.shape[2]
    step = jax.nn.softplus(dt_raw)
    logdec = -step * jnp.exp(a_log)[None, :]
    b_in = bc[:, :state].astype(jnp.float32)
    c_out = bc[:, state:].astype(jnp.float32)
    inputs = x.astype(jnp.float32).reshape(length, heads, width) * step[:, :, None]
    decays = jnp.transpose(logdec, (1, 0))
    rows = jnp.arange(length, dtype=jnp.int32)
    causal = rows[:, None] >= rows[None, :]
    cum = jnp.cumsum(decays, axis=1)
    diff = cum[:, :, None] - cum[:, None, :]
    weights = jnp.exp(jnp.where(causal[None, :, :], diff, -jnp.inf))
    scores = jnp.einsum("tn,sn->ts", c_out, b_in, precision=HIGH)
    mixing = weights * scores[None, :, :]
    y_intra = jnp.einsum("hts,shp->thp", mixing, inputs, precision=HIGH)
    ends = cum[:, -1]
    tail = jnp.transpose(jnp.exp(ends[:, None] - cum), (1, 0))
    fresh = jnp.einsum("shp,sn->hpn", inputs * tail[:, :, None], b_in, precision=HIGH)
    h_end = fresh + jnp.exp(ends)[:, None, None] * h_in
    y_inter = (
        jnp.einsum("tn,hpn->thp", c_out, h_in, precision=HIGH)
        * jnp.exp(jnp.transpose(cum, (1, 0)))[:, :, None]
    )
    return ((y_intra + y_inter).reshape(length, heads * width), h_end)


def per_device(hidden, w_bc, xs, dt_raw, a_log, d_out):
    tokens_here = hidden[0]
    channels = xs[0]
    step_raw = dt_raw[0]
    upstream = d_out[0].astype(jnp.float32)
    heads = a_log.shape[0]
    width = channels.shape[1] // heads
    state = w_bc.shape[1] // 2
    length = channels.shape[0]
    bc = jnp.dot(tokens_here, w_bc, preferred_element_type=jnp.float32).astype(jnp.bfloat16)
    step_sizes = jax.nn.softplus(step_raw)
    log_decay = -step_sizes * jnp.exp(a_log)[None, :]
    running = jnp.cumsum(log_decay, axis=0)
    b_rows = bc[:, :state].astype(jnp.float32)
    c_rows = bc[:, state:].astype(jnp.float32)
    tail_weight = jnp.exp(running[-1:, :] - running) * step_sizes
    weighted = channels.astype(jnp.float32).reshape(length, heads, width) * tail_weight[:, :, None]
    own_state = jnp.einsum("thp,tn->hpn", weighted, b_rows, precision=HIGH)
    scaled_grad = upstream.reshape(length, heads, width) * jnp.exp(running)[:, :, None]
    back_term = jnp.einsum("thp,tn->hpn", scaled_grad, c_rows, precision=HIGH)
    incoming, outgoing_grad = exchange(running[-1], own_state, back_term)

    def whole_block(bc_in, x_in, alog_in):
        return block_forward(bc_in, x_in, step_raw, alog_in, incoming)

    _, pull_all = jax.vjp(whole_block, bc, channels, a_log)
    d_bc, d_x, d_rate = pull_all((upstream, outgoing_grad))
    rows, cols = tokens_here.shape[1], d_bc.shape[1]
    half = rows // 2
    first = lax.axis_index("core") == 0
    top, bottom = tokens_here[:, :half], tokens_here[:, half:]
    dims = (((0,), (0,)), ((), ()))
    keep = lax.dot_general(jnp.where(first, top, bottom), d_bc, dims, preferred_element_type=jnp.float32)
    give = lax.dot_general(jnp.where(first, bottom, top), d_bc, dims, preferred_element_type=jnp.float32)
    rate_rows = jnp.zeros((8, cols), jnp.float32).at[0, :heads].set(d_rate)
    swap = [(0, 1), (1, 0)]
    paired = keep + lax.ppermute(give, "core", swap)
    rate_pair = rate_rows + lax.ppermute(rate_rows, "core", swap)
    axes = ("cz", "dp")
    total = lax.axis_size(axes)
    chunk = half // total
    parcel = jnp.concatenate(
        [paired.reshape(total, chunk, cols), jnp.broadcast_to(rate_pair[None], (total, 8, cols))], axis=1
    )
    pieces = lax.all_to_all(parcel, axes, 0, 0, tiled=True)
    mine_sum = jnp.sum(pieces, axis=0)
    spread = jnp.broadcast_to(mine_sum[None, :chunk], (total, chunk, cols))
    own_half = lax.all_to_all(spread, axes, 0, 0, tiled=True).reshape(half, cols)
    other_half = lax.ppermute(own_half, "core", swap)
    d_wbc = jnp.concatenate(
        [jnp.where(first, own_half, other_half), jnp.where(first, other_half, own_half)], axis=0
    )
    d_alog = mine_sum[chunk, :heads]
    return (d_x[None], d_wbc, d_alog)


def solution(mesh):
    rows, dp = mesh.devices.shape
    split = Mesh(mesh.devices.reshape(rows // 2, 2, dp), ("cz", "core", "dp"))
    blocks = P("dp", CHAIN, None)
    return jax.shard_map(
        per_device,
        mesh=split,
        in_specs=(blocks, P(), blocks, blocks, P(), blocks),
        out_specs=(blocks, P(), P()),
        check_vma=False,
    )
```

```python
import jax
import jax.numpy as jnp
from jax import lax
from jax.sharding import Mesh, PartitionSpec as P

GROUP = 128
CHAIN = ("cz", "core")


HIGH = lax.Precision.HIGH


def exchange(log_total, own_state, back_term):
    heads, width, state = own_state.shape
    first = lax.axis_index("core") == 0
    swap = [(0, 1), (1, 0)]

    def marked(value, logs):
        return jnp.concatenate([value, jnp.broadcast_to(logs[:, None, None], (heads, 8, state))], axis=1)

    ahead = lax.ppermute(marked(own_state, log_total), "core", [(0, 1)])
    behind = lax.ppermute(marked(back_term, log_total), "core", [(1, 0)])
    got = jnp.where(first, behind, ahead)
    partner = got[:, :width]
    partner_log = got[:, width, 0]
    pair_log = log_total + partner_log
    mine = jnp.where(first, back_term, own_state)
    combined = mine + jnp.exp(log_total)[:, None, None] * partner
    count = lax.axis_size("cz")
    per = heads // count
    sent = lax.all_to_all(marked(combined, pair_log), "cz", 0, 0, tiled=True).reshape(count, per, width + 8, state)
    chip_logs = sent[:, :, width, 0]
    edge = jnp.cumsum(chip_logs, axis=0) - chip_logs
    after = edge + chip_logs
    pos = jnp.arange(count, dtype=jnp.int32)
    earlier = pos[None, :] < pos[:, None]
    fwd_w = jnp.exp(jnp.where(earlier[:, :, None], edge[:, None, :] - after[None, :, :], -jnp.inf))
    bwd_w = jnp.exp(jnp.where(earlier.T[:, :, None], edge[None, :, :] - after[:, None, :], -jnp.inf))
    weight = jnp.where(first, bwd_w, fwd_w)
    res = jnp.einsum("djh,jhpn->dhpn", weight, sent, precision=HIGH).reshape(count * per, width + 8, state)
    back = lax.all_to_all(res, "cz", 0, 0, tiled=True)
    other = lax.ppermute(back, "core", swap)[:, :width]
    fixed = jnp.exp(partner_log)[:, None, None] * back[:, :width] + partner
    return jnp.where(first, other, fixed), jnp.where(first, fixed, other)


def block_forward(bc, x, dt_raw, a_log, h_in):
    length = x.shape[0]
    heads = h_in.shape[0]
    width = h_in.shape[1]
    state = h_in.shape[2]
    step = jax.nn.softplus(dt_raw)
    logdec = -step * jnp.exp(a_log)[None, :]
    b_in = bc[:, :state].astype(jnp.float32)
    c_out = bc[:, state:].astype(jnp.float32)
    inputs = x.astype(jnp.float32).reshape(length, heads, width) * step[:, :, None]
    decays = jnp.transpose(logdec, (1, 0))
    rows = jnp.arange(length, dtype=jnp.int32)
    causal = rows[:, None] >= rows[None, :]
    cum = jnp.cumsum(decays, axis=1)
    diff = cum[:, :, None] - cum[:, None, :]
    weights = jnp.exp(jnp.where(causal[None, :, :], diff, -jnp.inf))
    scores = jnp.einsum("tn,sn->ts", c_out, b_in, precision=HIGH)
    mixing = weights * scores[None, :, :]
    y_intra = jnp.einsum("hts,shp->thp", mixing, inputs, precision=HIGH)
    ends = cum[:, -1]
    tail = jnp.transpose(jnp.exp(ends[:, None] - cum), (1, 0))
    fresh = jnp.einsum("shp,sn->hpn", inputs * tail[:, :, None], b_in, precision=HIGH)
    h_end = fresh + jnp.exp(ends)[:, None, None] * h_in
    y_inter = (
        jnp.einsum("tn,hpn->thp", c_out, h_in, precision=HIGH)
        * jnp.exp(jnp.transpose(cum, (1, 0)))[:, :, None]
    )
    return ((y_intra + y_inter).reshape(length, heads * width), h_end)


def per_device(hidden, w_bc, xs, dt_raw, a_log, d_out):
    tokens_here = hidden[0]
    channels = xs[0]
    step_raw = dt_raw[0]
    upstream = d_out[0].astype(jnp.float32)
    heads = a_log.shape[0]
    width = channels.shape[1] // heads
    state = w_bc.shape[1] // 2
    length = channels.shape[0]
    bc = jnp.dot(tokens_here, w_bc, preferred_element_type=jnp.float32).astype(jnp.bfloat16)
    step_sizes = jax.nn.softplus(step_raw)
    log_decay = -step_sizes * jnp.exp(a_log)[None, :]
    running = jnp.cumsum(log_decay, axis=0)
    b_rows = bc[:, :state].astype(jnp.float32)
    c_rows = bc[:, state:].astype(jnp.float32)
    tail_weight = jnp.exp(running[-1:, :] - running) * step_sizes
    weighted = channels.astype(jnp.float32).reshape(length, heads, width) * tail_weight[:, :, None]
    own_state = jnp.einsum("thp,tn->hpn", weighted, b_rows, precision=HIGH)
    scaled_grad = upstream.reshape(length, heads, width) * jnp.exp(running)[:, :, None]
    back_term = jnp.einsum("thp,tn->hpn", scaled_grad, c_rows, precision=HIGH)
    incoming, outgoing_grad = exchange(running[-1], own_state, back_term)

    def whole_block(bc_in, x_in, alog_in):
        return block_forward(bc_in, x_in, step_raw, alog_in, incoming)

    _, pull_all = jax.vjp(whole_block, bc, channels, a_log)
    d_bc, d_x, d_rate = pull_all((upstream, outgoing_grad))
    rows, cols = tokens_here.shape[1], d_bc.shape[1]
    half = rows // 2
    first = lax.axis_index("core") == 0
    top, bottom = tokens_here[:, :half], tokens_here[:, half:]
    dims = (((0,), (0,)), ((), ()))
    keep = lax.dot_general(jnp.where(first, top, bottom), d_bc, dims, preferred_element_type=jnp.float32)
    give = lax.dot_general(jnp.where(first, bottom, top), d_bc, dims, preferred_element_type=jnp.float32)
    rate_rows = jnp.zeros((8, cols), jnp.float32).at[0, :heads].set(d_rate)
    swap = [(0, 1), (1, 0)]
    paired = keep + lax.ppermute(give, "core", swap)
    rate_pair = rate_rows + lax.ppermute(rate_rows, "core", swap)
    axes = ("cz", "dp")
    total = lax.axis_size(axes)
    chunk = half // total
    parcel = jnp.concatenate(
        [paired.reshape(total, chunk, cols), jnp.broadcast_to(rate_pair[None], (total, 8, cols))], axis=1
    )
    pieces = lax.all_to_all(parcel, axes, 0, 0, tiled=True)
    mine_sum = jnp.sum(pieces, axis=0)
    spread = jnp.broadcast_to(mine_sum[None, :chunk], (total, chunk, cols))
    own_half = lax.all_to_all(spread, axes, 0, 0, tiled=True).reshape(half, cols)
    other_half = lax.ppermute(own_half, "core", swap)
    d_wbc = jnp.concatenate(
        [jnp.where(first, own_half, other_half), jnp.where(first, other_half, own_half)], axis=0
    )
    d_alog = mine_sum[chunk, :heads]
    return (d_x[None], d_wbc, d_alog)


def solution(mesh):
    rows, dp = mesh.devices.shape
    split = Mesh(mesh.devices.reshape(rows // 2, 2, dp), ("cz", "core", "dp"))
    blocks = P("dp", CHAIN, None)
    return jax.shard_map(
        per_device,
        mesh=split,
        in_specs=(blocks, P(), blocks, blocks, P(), blocks),
        out_specs=(blocks, P(), P()),
        check_vma=False,
    )
```

```python
import jax
import jax.numpy as jnp
from jax import lax
from jax.sharding import Mesh, PartitionSpec as P

GROUP = 128
CHAIN = ("cz", "core")


HIGH = lax.Precision.HIGH


def exchange(log_total, own_state, back_term):
    heads, width, state = own_state.shape
    first = lax.axis_index("core") == 0
    swap = [(0, 1), (1, 0)]

    def marked(value, logs):
        return jnp.concatenate([value, jnp.broadcast_to(logs[:, None, None], (heads, 8, state))], axis=1)

    got = lax.ppermute(marked(jnp.where(first, own_state, back_term), log_total), "core", swap)
    partner = got[:, :width]
    partner_log = got[:, width, 0]
    pair_log = log_total + partner_log
    mine = jnp.where(first, back_term, own_state)
    combined = mine + jnp.exp(log_total)[:, None, None] * partner
    count = lax.axis_size("cz")
    per = heads // count
    sent = lax.all_to_all(marked(combined, pair_log), "cz", 0, 0, tiled=True).reshape(count, per, width + 8, state)
    chip_logs = sent[:, :, width, 0]
    edge = jnp.cumsum(chip_logs, axis=0) - chip_logs
    after = edge + chip_logs
    pos = jnp.arange(count, dtype=jnp.int32)
    earlier = pos[None, :] < pos[:, None]
    fwd_w = jnp.exp(jnp.where(earlier[:, :, None], edge[:, None, :] - after[None, :, :], -jnp.inf))
    bwd_w = jnp.exp(jnp.where(earlier.T[:, :, None], edge[None, :, :] - after[:, None, :], -jnp.inf))
    weight = jnp.where(first, bwd_w, fwd_w)
    res = jnp.einsum("djh,jhpn->dhpn", weight, sent, precision=HIGH).reshape(count * per, width + 8, state)
    back = lax.all_to_all(res, "cz", 0, 0, tiled=True)
    other = lax.ppermute(back, "core", swap)[:, :width]
    fixed = jnp.exp(partner_log)[:, None, None] * back[:, :width] + partner
    return jnp.where(first, other, fixed), jnp.where(first, fixed, other)


def block_forward(bc, x, dt_raw, a_log, h_in):
    length = x.shape[0]
    heads = h_in.shape[0]
    width = h_in.shape[1]
    state = h_in.shape[2]
    step = jax.nn.softplus(dt_raw)
    logdec = -step * jnp.exp(a_log)[None, :]
    b_in = bc[:, :state].astype(jnp.float32)
    c_out = bc[:, state:].astype(jnp.float32)
    inputs = x.astype(jnp.float32).reshape(length, heads, width) * step[:, :, None]
    decays = jnp.transpose(logdec, (1, 0))
    rows = jnp.arange(length, dtype=jnp.int32)
    causal = rows[:, None] >= rows[None, :]
    cum = jnp.cumsum(decays, axis=1)
    diff = cum[:, :, None] - cum[:, None, :]
    weights = jnp.exp(jnp.where(causal[None, :, :], diff, -jnp.inf))
    scores = jnp.einsum("tn,sn->ts", c_out, b_in, precision=HIGH)
    mixing = weights * scores[None, :, :]
    y_intra = jnp.einsum("hts,shp->thp", mixing, inputs, precision=HIGH)
    ends = cum[:, -1]
    tail = jnp.transpose(jnp.exp(ends[:, None] - cum), (1, 0))
    fresh = jnp.einsum("shp,sn->hpn", inputs * tail[:, :, None], b_in, precision=HIGH)
    h_end = fresh + jnp.exp(ends)[:, None, None] * h_in
    y_inter = (
        jnp.einsum("tn,hpn->thp", c_out, h_in, precision=HIGH)
        * jnp.exp(jnp.transpose(cum, (1, 0)))[:, :, None]
    )
    return ((y_intra + y_inter).reshape(length, heads * width), h_end)


def per_device(hidden, w_bc, xs, dt_raw, a_log, d_out):
    tokens_here = hidden[0]
    channels = xs[0]
    step_raw = dt_raw[0]
    upstream = d_out[0].astype(jnp.float32)
    heads = a_log.shape[0]
    width = channels.shape[1] // heads
    state = w_bc.shape[1] // 2
    length = channels.shape[0]
    bc = jnp.dot(tokens_here, w_bc, preferred_element_type=jnp.float32).astype(jnp.bfloat16)
    step_sizes = jax.nn.softplus(step_raw)
    log_decay = -step_sizes * jnp.exp(a_log)[None, :]
    running = jnp.cumsum(log_decay, axis=0)
    b_rows = bc[:, :state].astype(jnp.float32)
    c_rows = bc[:, state:].astype(jnp.float32)
    tail_weight = jnp.exp(running[-1:, :] - running) * step_sizes
    weighted = channels.astype(jnp.float32).reshape(length, heads, width) * tail_weight[:, :, None]
    own_state = jnp.einsum("thp,tn->hpn", weighted, b_rows, precision=HIGH)
    scaled_grad = upstream.reshape(length, heads, width) * jnp.exp(running)[:, :, None]
    back_term = jnp.einsum("thp,tn->hpn", scaled_grad, c_rows, precision=HIGH)
    incoming, outgoing_grad = exchange(running[-1], own_state, back_term)

    def whole_block(bc_in, x_in, alog_in):
        return block_forward(bc_in, x_in, step_raw, alog_in, incoming)

    _, pull_all = jax.vjp(whole_block, bc, channels, a_log)
    d_bc, d_x, d_rate = pull_all((upstream, outgoing_grad))
    rows, cols = tokens_here.shape[1], d_bc.shape[1]
    half = rows // 2
    first = lax.axis_index("core") == 0
    top, bottom = tokens_here[:, :half], tokens_here[:, half:]
    dims = (((0,), (0,)), ((), ()))
    keep = lax.dot_general(jnp.where(first, top, bottom), d_bc, dims, preferred_element_type=jnp.float32)
    give = lax.dot_general(jnp.where(first, bottom, top), d_bc, dims, preferred_element_type=jnp.float32)
    rate_rows = jnp.zeros((8, cols), jnp.float32).at[0, :heads].set(d_rate)
    swap = [(0, 1), (1, 0)]
    paired = keep + lax.ppermute(give, "core", swap)
    axes = ("cz", "dp")
    total = lax.axis_size(axes)
    chunk = half // total
    parcel = jnp.concatenate(
        [paired.reshape(total, chunk, cols), jnp.broadcast_to(rate_rows[None], (total, 8, cols))], axis=1
    )
    pieces = lax.all_to_all(parcel, axes, 0, 0, tiled=True)
    mine_sum = jnp.sum(pieces, axis=0)
    spread = jnp.broadcast_to(mine_sum[None, :chunk], (total, chunk, cols))
    own_half = lax.all_to_all(spread, axes, 0, 0, tiled=True).reshape(half, cols)
    other_half = lax.ppermute(own_half, "core", swap)
    d_wbc = jnp.concatenate(
        [jnp.where(first, own_half, other_half), jnp.where(first, other_half, own_half)], axis=0
    )
    partial = mine_sum[chunk, :heads]
    d_alog = partial + lax.ppermute(partial, "core", swap)
    return (d_x[None], d_wbc, d_alog)


def solution(mesh):
    rows, dp = mesh.devices.shape
    split = Mesh(mesh.devices.reshape(rows // 2, 2, dp), ("cz", "core", "dp"))
    blocks = P("dp", CHAIN, None)
    return jax.shard_map(
        per_device,
        mesh=split,
        in_specs=(blocks, P(), blocks, blocks, P(), blocks),
        out_specs=(blocks, P(), P()),
        check_vma=False,
    )
```
